128 devices in a mesh: scen: 8 (over y, x_lo), gx: 4 (over x_hi, core), gy: 4 (over z).
Axes of the slice: x: 4 (x_hi: 2, x_lo: 2; x = x_hi * 2 + x_lo), y: 4, z: 4, core: 2. Of those that a mesh axis runs over, the one named last changes fastest.
Arguments:
- source: float32 [8, 32, 1024, 1024], P('scen', None, 'gx', 'gy'), may hold values from 0.2 to 3
- obstacle: int32 [32, 1024, 1024], P(None, 'gx', 'gy'), may hold values 0 or 1
- sector: int32 [8], P('scen'), may hold values from 0 to 15
- freq_class: int32 [8], P('scen'), may hold values from 0 to 4
Outputs:
- risk: float32 [16, 1024, 1024], P('scen', 'gx', 'gy')
The draws below stay inside these ranges and needn't reach their ends.
All inputs are finite; a program needn't handle non-finite values. No bound on the sum of `obstacle` on one device may be relied on, other than what follows from the above.
Results may differ from the reference program's by a relative error of at most 0.00002.
Values sent between devices are 32-bit elements; how exact they have to be, the bound alone decides.
No kernel may reach another device: no remote copies, remote signals or barrier semaphores. Data moves between devices by JAX's collectives and lax.ppermute only.
A program may use at most 256 MiB of HBM per device.

```python
import math
import jax
import jax.numpy as jnp
from jax import lax

NZ = 32
STEPS = 4
RZ = 16
SCEN = 8
NX = 1024
NY = 1024


def plant(array, rng, least, high):
    dims = array.shape
    index_at = [jax.random.randint(jax.random.fold_in(rng, axis), (), 0, dims[axis]) for axis in range(len(dims))]
    array = array.at[tuple(index_at)].set(least)
    longest = dims.index(max(dims))
    index_at[longest] = (index_at[longest] + 1) % dims[longest]
    return array.at[tuple(index_at)].set(high)


def levels(stream_key, dims, pieces, low, largest):
    def one(position, parts):
        draws = jax.random.uniform(jax.random.fold_in(jax.random.fold_in(stream_key, 6), position), (parts,), jnp.float32, low / len(pieces), largest / len(pieces))
        return jnp.repeat(jnp.exp(draws), dims[position] // parts).reshape((-1,) + (1,) * (len(dims) - position - 1))

    gain = one(*pieces[0])
    for cut in pieces[1:]:
        gain = gain * one(*cut)
    return gain


def setup_inputs(seed: int = 0) -> dict:
    seeds = jax.random.split(jax.random.key(seed), 5)
    source = jnp.clip(0.2 + 2.8 * jax.random.uniform(seeds[0], (SCEN, NZ, NX, NY), jnp.float32) ** levels(seeds[0], (SCEN, NZ, NX, NY), ((0, 8), (2, 4), (3, 4)), -0.2, 0.2), 0.2, 3.0)
    obstacle = plant((jax.random.randint(seeds[1], (NZ, NX, NY), 0, 5) < 1).astype(jnp.int32), jax.random.fold_in(seeds[1], 1), 0, 1)
    sector = plant(jax.random.randint(seeds[2], (SCEN,), 0, 16), jax.random.fold_in(seeds[2], 1), 0, 15).astype(jnp.int32)
    freq_class = plant(jax.random.randint(seeds[3], (SCEN,), 0, 5), jax.random.fold_in(seeds[3], 1), 0, 4).astype(jnp.int32)
    return {"source": source, "obstacle": obstacle, "sector": sector, "freq_class": freq_class}


wind_speed = 0.4
diffusion = 0.05
settling = 0.1
probit_a = 3.0
probit_b = 1.0
load_eps = 0.01
freq_rate = 0.7

def wind_components(sector_id):
    heading = sector_id.astype(jnp.float32) * (2.0 * math.pi / 16.0)
    return (wind_speed * jnp.cos(heading), wind_speed * jnp.sin(heading))

def advance(padded, open_cells, courant_x, courant_y):
    centre = padded[:, 1:-1, 1:-1]
    west_side = padded[:, :-2, 1:-1]
    east_side = padded[:, 2:, 1:-1]
    south_side = padded[:, 1:-1, :-2]
    north_side = padded[:, 1:-1, 2:]
    zero_plane = jnp.zeros_like(centre[:1])
    upper_cell = jnp.concatenate([centre[1:], zero_plane], 0)
    lower_cell = jnp.concatenate([centre[:1], centre[:-1]], 0)
    falling = jnp.concatenate([zero_plane, centre[1:]], 0)
    advect = jnp.maximum(courant_x, 0.0) * (centre - west_side) + jnp.minimum(courant_x, 0.0) * (east_side - centre)
    advect = advect + jnp.maximum(courant_y, 0.0) * (centre - south_side) + jnp.minimum(courant_y, 0.0) * (north_side - centre)
    spread = west_side + east_side + south_side + north_side + upper_cell + lower_cell - 6.0 * centre
    return (centre - advect + diffusion * spread + settling * (upper_cell - falling)) * open_cells

def lethality(toxic_load):
    probit = probit_a + probit_b * jnp.log(toxic_load + load_eps)
    return 0.5 * (1.0 + lax.erf((probit - 5.0) / math.sqrt(2.0)))

def reference(source, obstacle, sector, freq_class):
    open_cells = (1 - obstacle).astype(jnp.float32)
    weights = jnp.exp(-freq_rate * freq_class.astype(jnp.float32))

    def one_scenario(summed, inputs):
        release, sector_id, weight = inputs
        courant_x, courant_y = wind_components(sector_id)
        current = release * open_cells
        toxic_load = jnp.zeros_like(current)
        for step_index in range(STEPS):
            padded = jnp.pad(current, ((0, 0), (1, 1), (1, 1)))
            current = advance(padded, open_cells, courant_x, courant_y)
            toxic_load = toxic_load + current * current
        return (summed + weight * lethality(toxic_load[:RZ]), None)
    start = jnp.zeros((RZ, NX, NY), jnp.float32)
    summed, unused = lax.scan(one_scenario, start, (source, sector, weights))
    return summed
```

```python
import math

import jax
import jax.numpy as jnp
from jax import lax
from jax.sharding import PartitionSpec as P

STEPS = 4
RZ = 16


wind_speed = 0.4
diffusion = 0.05
settling = 0.1
probit_a = 3.0
probit_b = 1.0
load_eps = 0.01
freq_rate = 0.7


def with_halo(block, sides, width):
    for axis, dim in sides:
        count = lax.axis_size(axis)
        forward = [(i, i + 1) for i in range(count - 1)]
        backward = [(target, source) for source, target in forward]
        low = lax.ppermute(
            lax.slice_in_dim(block, block.shape[dim] - width, None, axis=dim), axis, forward
        )
        high = lax.ppermute(lax.slice_in_dim(block, 0, width, axis=dim), axis, backward)
        block = jnp.concatenate([low, block, high], axis=dim)
    return block


def wind_components(sector_id):
    heading = sector_id.astype(jnp.float32) * (2.0 * math.pi / 16.0)
    return (wind_speed * jnp.cos(heading), wind_speed * jnp.sin(heading))


def advance(padded, open_cells, courant_x, courant_y):
    centre = padded[:, 1:-1, 1:-1]
    west_side = padded[:, :-2, 1:-1]
    east_side = padded[:, 2:, 1:-1]
    south_side = padded[:, 1:-1, :-2]
    north_side = padded[:, 1:-1, 2:]
    zero_plane = jnp.zeros_like(centre[:1])
    upper_cell = jnp.concatenate([centre[1:], zero_plane], 0)
    lower_cell = jnp.concatenate([centre[:1], centre[:-1]], 0)
    falling = jnp.concatenate([zero_plane, centre[1:]], 0)
    advect = jnp.maximum(courant_x, 0.0) * (centre - west_side) + jnp.minimum(courant_x, 0.0) * (
        east_side - centre
    )
    advect = (
        advect
        + jnp.maximum(courant_y, 0.0) * (centre - south_side)
        + jnp.minimum(courant_y, 0.0) * (north_side - centre)
    )
    spread = (
        west_side + east_side + south_side + north_side + upper_cell + lower_cell - 6.0 * centre
    )
    return (centre - advect + diffusion * spread + settling * (upper_cell - falling)) * open_cells


def lethality(toxic_load):
    probit = probit_a + probit_b * jnp.log(toxic_load + load_eps)
    return 0.5 * (1.0 + lax.erf((probit - 5.0) / math.sqrt(2.0)))


def on_device(source, obstacle, sector, freq_class):
    open_cells = (1 - obstacle).astype(jnp.float32)
    courant_x, courant_y = wind_components(sector[0])
    weight = jnp.exp(-freq_rate * freq_class[0].astype(jnp.float32))
    current = source[0] * open_cells
    toxic_load = jnp.zeros_like(current)
    for step_index in range(STEPS):
        padded = with_halo(current, (("gx", 1), ("gy", 2)), 1)
        current = advance(padded, open_cells, courant_x, courant_y)
        toxic_load = toxic_load + current * current
    weighted = weight * lethality(toxic_load[:RZ])
    return lax.psum_scatter(weighted, "scen", scatter_dimension=0, tiled=True)


def solution(mesh):
    in_specs = (P("scen", None, "gx", "gy"), P(None, "gx", "gy"), P("scen"), P("scen"))
    out_specs = P("scen", "gx", "gy")
    return jax.shard_map(
        on_device, mesh=mesh, in_specs=in_specs, out_specs=out_specs, check_vma=False
    )
```

```python
import math

import jax
import jax.numpy as jnp
from jax import lax
from jax.experimental import pallas as pl
from jax.experimental.pallas import tpu as pltpu
from jax.sharding import PartitionSpec as P

STEPS = 4
RZ = 16


wind_speed = 0.4
diffusion = 0.05
settling = 0.1
probit_a = 3.0
probit_b = 1.0
load_eps = 0.01
freq_rate = 0.7

H = STEPS
PAD = 16
EXTRA = 128
RB = 8


def wind_components(sector_id):
    heading = sector_id.astype(jnp.float32) * (2.0 * math.pi / 16.0)
    return (wind_speed * jnp.cos(heading), wind_speed * jnp.sin(heading))


def _open_and_c(src, obs):
    open_cells = (1 - obs).astype(jnp.float32)
    return jnp.stack([src * open_cells, open_cells])


def ghost_pieces(src, obs):
    nz, nx, ny = src.shape
    gxn = lax.axis_size("gx")
    gyn = lax.axis_size("gy")
    fx = [(i, i + 1) for i in range(gxn - 1)]
    bx = [(i + 1, i) for i in range(gxn - 1)]
    fy = [(i, i + 1) for i in range(gyn - 1)]
    by = [(i + 1, i) for i in range(gyn - 1)]
    last_rows = _open_and_c(src[:, nx - H:, :], obs[:, nx - H:, :])
    first_rows = _open_and_c(src[:, :H, :], obs[:, :H, :])
    xlo = lax.ppermute(last_rows, "gx", fx)
    xhi = lax.ppermute(first_rows, "gx", bx)
    last_cols = _open_and_c(src[:, :, ny - H:], obs[:, :, ny - H:])
    first_cols = _open_and_c(src[:, :, :H], obs[:, :, :H])
    ext_last = jnp.concatenate([xlo[..., ny - H:], last_cols, xhi[..., ny - H:]], axis=2)
    ext_first = jnp.concatenate([xlo[..., :H], first_cols, xhi[..., :H]], axis=2)
    yw = lax.ppermute(jnp.swapaxes(ext_last, -1, -2), "gy", fy)
    ye = lax.ppermute(jnp.swapaxes(ext_first, -1, -2), "gy", by)
    yw = jnp.swapaxes(yw, -1, -2)
    ye = jnp.swapaxes(ye, -1, -2)
    rows = nx + 2 * PAD
    mid = jnp.zeros(ye.shape[:-1] + (EXTRA - 2 * H,), jnp.float32)
    lanes = jnp.concatenate([ye, mid, yw], axis=-1)
    lanes = jnp.pad(lanes, ((0, 0), (0, 0), (PAD - H, rows - nx - PAD - H), (0, 0)))
    r_lo = jnp.pad(xlo, ((0, 0), (0, 0), (PAD - H, 0), (0, 0)))
    r_hi = jnp.pad(xhi, ((0, 0), (0, 0), (0, PAD - H), (0, 0)))
    return r_lo, r_hi, lanes


def make_kernel(nz, nx, ny, rz):
    rows = nx + 2 * PAD
    width = ny + EXTRA
    nblk = rows // RB
    b_first = 1
    b_last = nblk - 2
    acc_lo = PAD // RB
    acc_hi = (PAD + nx) // RB

    def kernel(coef, src_hbm, obs_hbm, rlo_hbm, rhi_hbm, lanes_hbm, out_ref,
               a_buf, b_buf, o_buf, obs_buf, sems):
        copies = [
            pltpu.make_async_copy(obs_hbm, obs_buf, sems.at[0]),
            pltpu.make_async_copy(rlo_hbm.at[1], o_buf.at[:, pl.ds(0, PAD), pl.ds(0, ny)], sems.at[1]),
            pltpu.make_async_copy(rhi_hbm.at[1], o_buf.at[:, pl.ds(PAD + nx, PAD), pl.ds(0, ny)], sems.at[2]),
            pltpu.make_async_copy(lanes_hbm.at[1], o_buf.at[:, :, pl.ds(ny, EXTRA)], sems.at[3]),
            pltpu.make_async_copy(src_hbm.at[0], a_buf.at[:, pl.ds(PAD, nx), pl.ds(0, ny)], sems.at[4]),
            pltpu.make_async_copy(rlo_hbm.at[0], a_buf.at[:, pl.ds(0, PAD), pl.ds(0, ny)], sems.at[5]),
            pltpu.make_async_copy(rhi_hbm.at[0], a_buf.at[:, pl.ds(PAD + nx, PAD), pl.ds(0, ny)], sems.at[6]),
            pltpu.make_async_copy(lanes_hbm.at[0], a_buf.at[:, :, pl.ds(ny, EXTRA)], sems.at[7]),
        ]
        for cp in copies:
            cp.start()

        zeros = jnp.zeros((RB, width), jnp.float32)

        def clear(z, c):
            b_buf[z, pl.ds(0, RB), :] = zeros
            b_buf[z, pl.ds(rows - RB, RB), :] = zeros
            return c

        lax.fori_loop(0, nz, clear, 0)

        copies[0].wait()

        def to_open(z, c):
            o_buf[z, pl.ds(PAD, nx), pl.ds(0, ny)] = (1 - obs_buf[z]).astype(jnp.float32)
            return c

        lax.fori_loop(0, nz, to_open, 0)
        copies[4].wait()

        def to_c0(z, c):
            a_buf[z, pl.ds(PAD, nx), pl.ds(0, ny)] = (
                a_buf[z, pl.ds(PAD, nx), pl.ds(0, ny)] * o_buf[z, pl.ds(PAD, nx), pl.ds(0, ny)]
            )
            return c

        lax.fori_loop(0, nz, to_c0, 0)
        for cp in copies[1:4] + copies[5:]:
            cp.wait()

        k_w = coef[0]
        k_e = coef[1]
        k_s = coef[2]
        k_n = coef[3]
        k0_first = coef[4]
        k0_rest = coef[5]
        weight = coef[6]
        row_id = lax.broadcasted_iota(jnp.int32, (RB, width), 0)
        first_row = row_id == 0
        last_row = row_id == RB - 1

        def step(src, dst, first):
            def level(z, accumulate):
                zu = jnp.minimum(z + 1, nz - 1)
                zl = jnp.maximum(z - 1, 0)
                k0 = jnp.where(z == 0, k0_first, k0_rest)
                ku = jnp.where(z == nz - 1, 0.0, diffusion + settling).astype(jnp.float32)

                def blk(b, carry, acc):
                    prev, cur = carry
                    r = pl.multiple_of(b * RB, RB)
                    nxt = src[z, pl.ds(r + RB, RB), :]
                    west = jnp.where(first_row, pltpu.roll(prev, 1, 0), pltpu.roll(cur, 1, 0))
                    east = jnp.where(last_row, pltpu.roll(nxt, RB - 1, 0), pltpu.roll(cur, RB - 1, 0))
                    south = pltpu.roll(cur, 1, 1)
                    north = pltpu.roll(cur, width - 1, 1)
                    up = src[zu, pl.ds(r, RB), :]
                    low = src[zl, pl.ds(r, RB), :]
                    o = o_buf[z, pl.ds(r, RB), :]
                    new = o * (
                        k0 * cur
                        + k_w * west
                        + k_e * east
                        + k_s * south
                        + k_n * north
                        + ku * up
                        + diffusion * low
                    )
                    dst[z, pl.ds(r, RB), :] = new
                    if acc:
                        inner = new[:, :ny]
                        ro = pl.multiple_of(r - PAD, RB)
                        if first:
                            out_ref[z, pl.ds(ro, RB), :] = inner * inner
                        else:
                            out_ref[z, pl.ds(ro, RB), :] = out_ref[z, pl.ds(ro, RB), :] + inner * inner
                    return (cur, nxt)

                carry = (src[z, pl.ds(0, RB), :], src[z, pl.ds(RB, RB), :])
                if accumulate:
                    carry = lax.fori_loop(b_first, acc_lo, lambda b, c: blk(b, c, False), carry)
                    carry = lax.fori_loop(acc_lo, acc_hi, lambda b, c: blk(b, c, True), carry, unroll=4)
                    carry = lax.fori_loop(acc_hi, b_last + 1, lambda b, c: blk(b, c, False), carry)
                else:
                    carry = lax.fori_loop(b_first, b_last + 1, lambda b, c: blk(b, c, False), carry, unroll=2)

            def lvl_acc(z, c):
                level(z, True)
                return c

            def lvl_plain(z, c):
                level(z, False)
                return c

            lax.fori_loop(0, rz, lvl_acc, 0)
            lax.fori_loop(rz, nz, lvl_plain, 0)

        bufs = (a_buf, b_buf)
        for n in range(STEPS):
            step(bufs[n % 2], bufs[(n + 1) % 2], n == 0)

        def leth(z, c):
            for q in range(nx // 32):
                load = out_ref[z, pl.ds(q * 32, 32), :]
                probit = probit_a + probit_b * jnp.log(load + load_eps)
                lethal = 0.5 * (1.0 + lax.erf((probit - 5.0) / math.sqrt(2.0)))
                out_ref[z, pl.ds(q * 32, 32), :] = weight * lethal
            return c

        lax.fori_loop(0, rz, leth, 0)

    return kernel


def on_device(source, obstacle, sector, freq_class):
    src = source[0]
    nz, nx, ny = src.shape
    courant_x, courant_y = wind_components(sector[0])
    weight = jnp.exp(-freq_rate * freq_class[0].astype(jnp.float32))
    px = jnp.maximum(courant_x, 0.0)
    mx = jnp.minimum(courant_x, 0.0)
    py = jnp.maximum(courant_y, 0.0)
    my = jnp.minimum(courant_y, 0.0)
    base = 1.0 - px + mx - py + my - 6.0 * diffusion
    coef = jnp.stack(
        [px + diffusion, diffusion - mx, py + diffusion, diffusion - my, base, base - settling,
         weight, jnp.float32(0.0)]
    ).astype(jnp.float32)
    r_lo, r_hi, lanes = ghost_pieces(src, obstacle)
    rows = nx + 2 * PAD
    width = ny + EXTRA
    any_spec = pl.BlockSpec(memory_space=pl.ANY)
    weighted = pl.pallas_call(
        make_kernel(nz, nx, ny, RZ),
        out_shape=jax.ShapeDtypeStruct((RZ, nx, ny), jnp.float32),
        in_specs=[pl.BlockSpec(memory_space=pltpu.SMEM)] + [any_spec] * 5,
        out_specs=pl.BlockSpec(memory_space=pltpu.VMEM),
        scratch_shapes=[
            pltpu.VMEM((nz, rows, width), jnp.float32),
            pltpu.VMEM((nz, rows, width), jnp.float32),
            pltpu.VMEM((nz, rows, width), jnp.float32),
            pltpu.VMEM((nz, nx, ny), jnp.int32),
            pltpu.SemaphoreType.DMA((8,)),
        ],
        compiler_params=pltpu.CompilerParams(vmem_limit_bytes=62 * 1024 * 1024),
    )(coef, source, obstacle, r_lo, r_hi, lanes)
    return lax.psum_scatter(weighted, "scen", scatter_dimension=0, tiled=True)


def solution(mesh):
    in_specs = (P("scen", None, "gx", "gy"), P(None, "gx", "gy"), P("scen"), P("scen"))
    out_specs = P("scen", "gx", "gy")
    return jax.shard_map(
        on_device, mesh=mesh, in_specs=in_specs, out_specs=out_specs, check_vma=False
    )
```

```python
import math

import jax
import jax.numpy as jnp
from jax import lax
from jax.experimental import pallas as pl
from jax.experimental.pallas import tpu as pltpu
from jax.sharding import PartitionSpec as P

STEPS = 4
RZ = 16


wind_speed = 0.4
diffusion = 0.05
settling = 0.1
probit_a = 3.0
probit_b = 1.0
load_eps = 0.01
freq_rate = 0.7

H = STEPS
PAD = 16
EXTRA = 128
RB = 8


def wind_components(sector_id):
    heading = sector_id.astype(jnp.float32) * (2.0 * math.pi / 16.0)
    return (wind_speed * jnp.cos(heading), wind_speed * jnp.sin(heading))


def _open_and_c(src, obs):
    open_cells = (1 - obs).astype(jnp.float32)
    return jnp.stack([src * open_cells, open_cells])


def _select(count, width, picks):
    cols = jnp.asarray(picks, jnp.int32)[:, None]
    return (lax.broadcasted_iota(jnp.int32, (count, width), 1) == cols).astype(jnp.float32)


def ghost_pieces(src, obs):
    nz, nx, ny = src.shape
    gxn = lax.axis_size("gx")
    gyn = lax.axis_size("gy")
    fx = [(i, i + 1) for i in range(gxn - 1)]
    bx = [(i + 1, i) for i in range(gxn - 1)]
    fy = [(i, i + 1) for i in range(gyn - 1)]
    by = [(i + 1, i) for i in range(gyn - 1)]
    hi = lax.Precision.HIGHEST
    last_rows = _open_and_c(src[:, nx - H:, :], obs[:, nx - H:, :])
    first_rows = _open_and_c(src[:, :H, :], obs[:, :H, :])
    xlo = lax.ppermute(last_rows, "gx", fx)
    xhi = lax.ppermute(first_rows, "gx", bx)
    pick = _select(2 * H, ny, list(range(H)) + list(range(ny - H, ny)))
    src_cols = jnp.einsum("zxy,ky->zkx", src, pick, precision=hi)
    open_cols = jnp.einsum("zxy,ky->zkx", (1 - obs).astype(jnp.float32), pick, precision=hi)
    cols = jnp.stack([src_cols * open_cols, open_cols])
    corner_lo = jnp.swapaxes(jnp.concatenate([xlo[..., :H], xlo[..., ny - H:]], -1), -1, -2)
    corner_hi = jnp.swapaxes(jnp.concatenate([xhi[..., :H], xhi[..., ny - H:]], -1), -1, -2)
    ext = jnp.concatenate([corner_lo, cols, corner_hi], axis=-1)
    yw = lax.ppermute(ext[:, :, H:], "gy", fy)
    ye = lax.ppermute(ext[:, :, :H], "gy", by)
    rows = nx + 2 * PAD
    yt = jnp.concatenate([ye, yw], axis=2)
    yt = jnp.pad(yt, ((0, 0), (0, 0), (0, 0), (PAD - H, rows - nx - PAD - H)))
    place = _select(2 * H, EXTRA, list(range(H)) + list(range(EXTRA - H, EXTRA)))
    lanes = jnp.einsum("czkr,kj->czrj", yt, place, precision=hi)
    r_lo = jnp.pad(xlo, ((0, 0), (0, 0), (PAD - H, 0), (0, 0)))
    r_hi = jnp.pad(xhi, ((0, 0), (0, 0), (0, PAD - H), (0, 0)))
    return r_lo, r_hi, lanes


def make_kernel(nz, nx, ny, rz):
    rows = nx + 2 * PAD
    width = ny + EXTRA
    nblk = rows // RB
    b_first = 1
    b_last = nblk - 2
    acc_lo = PAD // RB
    acc_hi = (PAD + nx) // RB

    def kernel(coef, src_hbm, obs_hbm, rlo_hbm, rhi_hbm, lanes_hbm, out_ref,
               a_buf, b_buf, o_buf, obs_buf, sems):
        copies = [
            pltpu.make_async_copy(obs_hbm, obs_buf, sems.at[0]),
            pltpu.make_async_copy(rlo_hbm.at[1], o_buf.at[:, pl.ds(0, PAD), pl.ds(0, ny)], sems.at[1]),
            pltpu.make_async_copy(rhi_hbm.at[1], o_buf.at[:, pl.ds(PAD + nx, PAD), pl.ds(0, ny)], sems.at[2]),
            pltpu.make_async_copy(lanes_hbm.at[1], o_buf.at[:, :, pl.ds(ny, EXTRA)], sems.at[3]),
            pltpu.make_async_copy(src_hbm.at[0], a_buf.at[:, pl.ds(PAD, nx), pl.ds(0, ny)], sems.at[4]),
            pltpu.make_async_copy(rlo_hbm.at[0], a_buf.at[:, pl.ds(0, PAD), pl.ds(0, ny)], sems.at[5]),
            pltpu.make_async_copy(rhi_hbm.at[0], a_buf.at[:, pl.ds(PAD + nx, PAD), pl.ds(0, ny)], sems.at[6]),
            pltpu.make_async_copy(lanes_hbm.at[0], a_buf.at[:, :, pl.ds(ny, EXTRA)], sems.at[7]),
        ]
        for cp in copies:
            cp.start()

        zeros = jnp.zeros((RB, width), jnp.float32)

        def clear(z, c):
            b_buf[z, pl.ds(0, RB), :] = zeros
            b_buf[z, pl.ds(rows - RB, RB), :] = zeros
            return c

        lax.fori_loop(0, nz, clear, 0)

        copies[0].wait()

        def to_open(z, c):
            o_buf[z, pl.ds(PAD, nx), pl.ds(0, ny)] = (1 - obs_buf[z]).astype(jnp.float32)
            return c

        lax.fori_loop(0, nz, to_open, 0)
        copies[4].wait()

        def to_c0(z, c):
            a_buf[z, pl.ds(PAD, nx), pl.ds(0, ny)] = (
                a_buf[z, pl.ds(PAD, nx), pl.ds(0, ny)] * o_buf[z, pl.ds(PAD, nx), pl.ds(0, ny)]
            )
            return c

        lax.fori_loop(0, nz, to_c0, 0)
        for cp in copies[1:4] + copies[5:]:
            cp.wait()

        k_w = coef[0]
        k_e = coef[1]
        k_s = coef[2]
        k_n = coef[3]
        k0_first = coef[4]
        k0_rest = coef[5]
        weight = coef[6]
        row_id = lax.broadcasted_iota(jnp.int32, (RB, width), 0)
        first_row = row_id == 0
        last_row = row_id == RB - 1

        def step(src, dst, first):
            def level(z, accumulate):
                zu = jnp.minimum(z + 1, nz - 1)
                zl = jnp.maximum(z - 1, 0)
                k0 = jnp.where(z == 0, k0_first, k0_rest)
                ku = jnp.where(z == nz - 1, 0.0, diffusion + settling).astype(jnp.float32)

                def blk(b, carry, acc):
                    prev, cur = carry
                    r = pl.multiple_of(b * RB, RB)
                    nxt = src[z, pl.ds(r + RB, RB), :]
                    west = jnp.where(first_row, pltpu.roll(prev, 1, 0), pltpu.roll(cur, 1, 0))
                    east = jnp.where(last_row, pltpu.roll(nxt, RB - 1, 0), pltpu.roll(cur, RB - 1, 0))
                    south = pltpu.roll(cur, 1, 1)
                    north = pltpu.roll(cur, width - 1, 1)
                    up = src[zu, pl.ds(r, RB), :]
                    low = src[zl, pl.ds(r, RB), :]
                    o = o_buf[z, pl.ds(r, RB), :]
                    new = o * (
                        (k0 * cur + k_w * west)
                        + (k_e * east + k_s * south)
                        + ((k_n * north + ku * up) + diffusion * low)
                    )
                    dst[z, pl.ds(r, RB), :] = new
                    if acc:
                        inner = new[:, :ny]
                        ro = pl.multiple_of(r - PAD, RB)
                        if first:
                            out_ref[z, pl.ds(ro, RB), :] = inner * inner
                        else:
                            out_ref[z, pl.ds(ro, RB), :] = out_ref[z, pl.ds(ro, RB), :] + inner * inner
                    return (cur, nxt)

                carry = (src[z, pl.ds(0, RB), :], src[z, pl.ds(RB, RB), :])
                if accumulate:
                    carry = lax.fori_loop(b_first, acc_lo, lambda b, c: blk(b, c, False), carry)
                    carry = lax.fori_loop(acc_lo, acc_hi, lambda b, c: blk(b, c, True), carry, unroll=4)
                    carry = lax.fori_loop(acc_hi, b_last + 1, lambda b, c: blk(b, c, False), carry)
                else:
                    carry = lax.fori_loop(b_first, b_last + 1, lambda b, c: blk(b, c, False), carry, unroll=2)

            def lvl_acc(z, c):
                level(z, True)
                return c

            def lvl_plain(z, c):
                level(z, False)
                return c

            lax.fori_loop(0, rz, lvl_acc, 0)
            lax.fori_loop(rz, nz, lvl_plain, 0)

        bufs = (a_buf, b_buf)
        for n in range(STEPS):
            step(bufs[n % 2], bufs[(n + 1) % 2], n == 0)

        def leth(z, c):
            for q in range(nx // 32):
                load = out_ref[z, pl.ds(q * 32, 32), :]
                probit = probit_a + probit_b * jnp.log(load + load_eps)
                lethal = 0.5 * (1.0 + lax.erf((probit - 5.0) / math.sqrt(2.0)))
                out_ref[z, pl.ds(q * 32, 32), :] = weight * lethal
            return c

        lax.fori_loop(0, rz, leth, 0)

    return kernel


def on_device(source, obstacle, sector, freq_class):
    src = source[0]
    nz, nx, ny = src.shape
    courant_x, courant_y = wind_components(sector[0])
    weight = jnp.exp(-freq_rate * freq_class[0].astype(jnp.float32))
    px = jnp.maximum(courant_x, 0.0)
    mx = jnp.minimum(courant_x, 0.0)
    py = jnp.maximum(courant_y, 0.0)
    my = jnp.minimum(courant_y, 0.0)
    base = 1.0 - px + mx - py + my - 6.0 * diffusion
    coef = jnp.stack(
        [px + diffusion, diffusion - mx, py + diffusion, diffusion - my, base, base - settling,
         weight, jnp.float32(0.0)]
    ).astype(jnp.float32)
    r_lo, r_hi, lanes = ghost_pieces(src, obstacle)
    rows = nx + 2 * PAD
    width = ny + EXTRA
    any_spec = pl.BlockSpec(memory_space=pl.ANY)
    weighted = pl.pallas_call(
        make_kernel(nz, nx, ny, RZ),
        out_shape=jax.ShapeDtypeStruct((RZ, nx, ny), jnp.float32),
        in_specs=[pl.BlockSpec(memory_space=pltpu.SMEM)] + [any_spec] * 5,
        out_specs=pl.BlockSpec(memory_space=pltpu.VMEM),
        scratch_shapes=[
            pltpu.VMEM((nz, rows, width), jnp.float32),
            pltpu.VMEM((nz, rows, width), jnp.float32),
            pltpu.VMEM((nz, rows, width), jnp.float32),
            pltpu.VMEM((nz, nx, ny), jnp.int32),
            pltpu.SemaphoreType.DMA((8,)),
        ],
        compiler_params=pltpu.CompilerParams(vmem_limit_bytes=62 * 1024 * 1024),
    )(coef, source, obstacle, r_lo, r_hi, lanes)
    count = lax.axis_size("scen")
    parts = weighted.reshape(count, RZ // count, nx, ny)
    return lax.all_to_all(parts, "scen", 0, 0, tiled=True).sum(0)


def solution(mesh):
    in_specs = (P("scen", None, "gx", "gy"), P(None, "gx", "gy"), P("scen"), P("scen"))
    out_specs = P("scen", "gx", "gy")
    return jax.shard_map(
        on_device, mesh=mesh, in_specs=in_specs, out_specs=out_specs, check_vma=False
    )
```

```python
import math

import jax
import jax.numpy as jnp
from jax import lax
from jax.experimental import pallas as pl
from jax.experimental.pallas import tpu as pltpu
from jax.sharding import PartitionSpec as P

STEPS = 4
RZ = 16


wind_speed = 0.4
diffusion = 0.05
settling = 0.1
probit_a = 3.0
probit_b = 1.0
load_eps = 0.01
freq_rate = 0.7

H = STEPS
PAD = 16
EXTRA = 128
RB = 8
ROT_UNROLL = 34


def wind_components(sector_id):
    heading = sector_id.astype(jnp.float32) * (2.0 * math.pi / 16.0)
    return (wind_speed * jnp.cos(heading), wind_speed * jnp.sin(heading))


def _open_and_c(src, obs):
    open_cells = (1 - obs).astype(jnp.float32)
    return jnp.stack([src * open_cells, open_cells])


def _select(count, width, picks):
    cols = jnp.asarray(picks, jnp.int32)[:, None]
    return (lax.broadcasted_iota(jnp.int32, (count, width), 1) == cols).astype(jnp.float32)


def ghost_pieces(src, obs):
    nz, nx, ny = src.shape
    gxn = lax.axis_size("gx")
    gyn = lax.axis_size("gy")
    fx = [(i, i + 1) for i in range(gxn - 1)]
    bx = [(i + 1, i) for i in range(gxn - 1)]
    fy = [(i, i + 1) for i in range(gyn - 1)]
    by = [(i + 1, i) for i in range(gyn - 1)]
    hi = lax.Precision.HIGHEST
    last_rows = _open_and_c(src[:, nx - H:, :], obs[:, nx - H:, :])
    first_rows = _open_and_c(src[:, :H, :], obs[:, :H, :])
    xlo = lax.ppermute(last_rows, "gx", fx)
    xhi = lax.ppermute(first_rows, "gx", bx)
    pick = _select(2 * H, ny, list(range(H)) + list(range(ny - H, ny)))
    src_cols = jnp.einsum("zxy,ky->zkx", src, pick, precision=hi)
    open_cols = jnp.einsum("zxy,ky->zkx", (1 - obs).astype(jnp.float32), pick, precision=hi)
    cols = jnp.stack([src_cols * open_cols, open_cols])
    corner_lo = jnp.swapaxes(jnp.concatenate([xlo[..., :H], xlo[..., ny - H:]], -1), -1, -2)
    corner_hi = jnp.swapaxes(jnp.concatenate([xhi[..., :H], xhi[..., ny - H:]], -1), -1, -2)
    ext = jnp.concatenate([corner_lo, cols, corner_hi], axis=-1)
    yw = lax.ppermute(ext[:, :, H:], "gy", fy)
    ye = lax.ppermute(ext[:, :, :H], "gy", by)
    rows = nx + 2 * PAD
    yt = jnp.concatenate([ye, yw], axis=2)
    yt = jnp.pad(yt, ((0, 0), (0, 0), (0, 0), (PAD - H, rows - nx - PAD - H)))
    place = _select(2 * H, EXTRA, list(range(H)) + list(range(EXTRA - H, EXTRA)))
    lanes = jnp.einsum("czkr,kj->czrj", yt, place, precision=hi)
    r_lo = jnp.pad(xlo, ((0, 0), (0, 0), (PAD - H, 0), (0, 0)))
    r_hi = jnp.pad(xhi, ((0, 0), (0, 0), (0, PAD - H), (0, 0)))
    return r_lo, r_hi, lanes


def make_kernel(nz, nx, ny, rz):
    rows = nx + 2 * PAD
    width = ny + EXTRA
    nblk = rows // RB
    b_first = 1
    b_last = nblk - 2
    acc_lo = PAD // RB
    acc_hi = (PAD + nx) // RB

    def kernel(coef, src_hbm, obs_hbm, rlo_hbm, rhi_hbm, lanes_hbm, out_ref,
               a_buf, b_buf, o_buf, obs_buf, sems, s_buf, n_buf):
        copies = [
            pltpu.make_async_copy(obs_hbm, obs_buf, sems.at[0]),
            pltpu.make_async_copy(rlo_hbm.at[1], o_buf.at[:, pl.ds(0, PAD), pl.ds(0, ny)], sems.at[1]),
            pltpu.make_async_copy(rhi_hbm.at[1], o_buf.at[:, pl.ds(PAD + nx, PAD), pl.ds(0, ny)], sems.at[2]),
            pltpu.make_async_copy(lanes_hbm.at[1], o_buf.at[:, :, pl.ds(ny, EXTRA)], sems.at[3]),
            pltpu.make_async_copy(src_hbm.at[0], a_buf.at[:, pl.ds(PAD, nx), pl.ds(0, ny)], sems.at[4]),
            pltpu.make_async_copy(rlo_hbm.at[0], a_buf.at[:, pl.ds(0, PAD), pl.ds(0, ny)], sems.at[5]),
            pltpu.make_async_copy(rhi_hbm.at[0], a_buf.at[:, pl.ds(PAD + nx, PAD), pl.ds(0, ny)], sems.at[6]),
            pltpu.make_async_copy(lanes_hbm.at[0], a_buf.at[:, :, pl.ds(ny, EXTRA)], sems.at[7]),
        ]
        for cp in copies:
            cp.start()

        zeros = jnp.zeros((RB, width), jnp.float32)

        def clear(z, c):
            b_buf[z, pl.ds(0, RB), :] = zeros
            b_buf[z, pl.ds(rows - RB, RB), :] = zeros
            return c

        lax.fori_loop(0, nz, clear, 0)

        copies[0].wait()

        def to_open(z, c):
            o_buf[z, pl.ds(PAD, nx), pl.ds(0, ny)] = (1 - obs_buf[z]).astype(jnp.float32)
            return c

        lax.fori_loop(0, nz, to_open, 0)
        copies[4].wait()

        def to_c0(z, c):
            a_buf[z, pl.ds(PAD, nx), pl.ds(0, ny)] = (
                a_buf[z, pl.ds(PAD, nx), pl.ds(0, ny)] * o_buf[z, pl.ds(PAD, nx), pl.ds(0, ny)]
            )
            return c

        lax.fori_loop(0, nz, to_c0, 0)
        for cp in copies[1:4] + copies[5:]:
            cp.wait()

        k_w = coef[0]
        k_e = coef[1]
        k_s = coef[2]
        k_n = coef[3]
        k0_first = coef[4]
        k0_rest = coef[5]
        weight = coef[6]
        npc = width // 128
        nacc = ny // 128
        row_id = lax.broadcasted_iota(jnp.int32, (RB, 128), 0)
        lane_id = lax.broadcasted_iota(jnp.int32, (RB, 128), 1)
        first_row = row_id == 0
        last_row = row_id == RB - 1
        first_lane = lane_id == 0
        last_lane = lane_id == 127

        def pieces(ref, z, r):
            return tuple(ref[z, pl.ds(r, RB), pl.ds(128 * k, 128)] for k in range(npc))

        def step(src, dst, first):
            def level(z, accumulate):
                zu = jnp.minimum(z + 1, nz - 1)
                zl = jnp.maximum(z - 1, 0)
                k0 = jnp.where(z == 0, k0_first, k0_rest)
                ku = jnp.where(z == nz - 1, 0.0, diffusion + settling).astype(jnp.float32)

                def rot(b, c):
                    r = pl.multiple_of(b * RB, RB)
                    cur = pieces(src, z, r)
                    right = tuple(pltpu.roll(v, 1, 1) for v in cur)
                    left = tuple(pltpu.roll(v, 127, 1) for v in cur)
                    for k in range(npc):
                        s_buf[pl.ds(r, RB), pl.ds(128 * k, 128)] = jnp.where(
                            first_lane, right[(k - 1) % npc], right[k])
                        n_buf[pl.ds(r, RB), pl.ds(128 * k, 128)] = jnp.where(
                            last_lane, left[(k + 1) % npc], left[k])
                    return c

                lax.fori_loop(b_first, b_last + 1, rot, 0, unroll=ROT_UNROLL)

                def blk(b, carry, acc):
                    prev, cur = carry
                    r = pl.multiple_of(b * RB, RB)
                    nxt = pieces(src, z, r + RB)
                    up = pieces(src, zu, r)
                    low = pieces(src, zl, r)
                    o = pieces(o_buf, z, r)
                    ro = pl.multiple_of(r - PAD, RB)
                    for k in range(npc):
                        c = cur[k]
                        west = jnp.where(first_row, pltpu.roll(prev[k], 1, 0), pltpu.roll(c, 1, 0))
                        east = jnp.where(last_row, pltpu.roll(nxt[k], RB - 1, 0), pltpu.roll(c, RB - 1, 0))
                        south = s_buf[pl.ds(r, RB), pl.ds(128 * k, 128)]
                        north = n_buf[pl.ds(r, RB), pl.ds(128 * k, 128)]
                        new = o[k] * (
                            (k0 * c + k_w * west)
                            + (k_e * east + k_s * south)
                            + ((k_n * north + ku * up[k]) + diffusion * low[k])
                        )
                        dst[z, pl.ds(r, RB), pl.ds(128 * k, 128)] = new
                        if acc and k < nacc:
                            sq = new * new
                            if first:
                                out_ref[z, pl.ds(ro, RB), pl.ds(128 * k, 128)] = sq
                            else:
                                out_ref[z, pl.ds(ro, RB), pl.ds(128 * k, 128)] = (
                                    out_ref[z, pl.ds(ro, RB), pl.ds(128 * k, 128)] + sq
                                )
                    return (cur, nxt)

                carry = (pieces(src, z, 0), pieces(src, z, RB))
                if accumulate:
                    carry = lax.fori_loop(b_first, acc_lo, lambda b, c: blk(b, c, False), carry)
                    carry = lax.fori_loop(acc_lo, acc_hi, lambda b, c: blk(b, c, True), carry, unroll=4)
                    carry = lax.fori_loop(acc_hi, b_last + 1, lambda b, c: blk(b, c, False), carry)
                else:
                    carry = lax.fori_loop(b_first, b_last + 1, lambda b, c: blk(b, c, False), carry, unroll=2)

            def lvl_acc(z, c):
                level(z, True)
                return c

            def lvl_plain(z, c):
                level(z, False)
                return c

            lax.fori_loop(0, rz, lvl_acc, 0)
            lax.fori_loop(rz, nz, lvl_plain, 0)

        bufs = (a_buf, b_buf)
        for n in range(STEPS):
            step(bufs[n % 2], bufs[(n + 1) % 2], n == 0)

        def leth(z, c):
            for q in range(nx // 32):
                load = out_ref[z, pl.ds(q * 32, 32), :]
                probit = probit_a + probit_b * jnp.log(load + load_eps)
                lethal = 0.5 * (1.0 + lax.erf((probit - 5.0) / math.sqrt(2.0)))
                out_ref[z, pl.ds(q * 32, 32), :] = weight * lethal
            return c

        lax.fori_loop(0, rz, leth, 0)

    return kernel


def on_device(source, obstacle, sector, freq_class):
    src = source[0]
    nz, nx, ny = src.shape
    courant_x, courant_y = wind_components(sector[0])
    weight = jnp.exp(-freq_rate * freq_class[0].astype(jnp.float32))
    px = jnp.maximum(courant_x, 0.0)
    mx = jnp.minimum(courant_x, 0.0)
    py = jnp.maximum(courant_y, 0.0)
    my = jnp.minimum(courant_y, 0.0)
    base = 1.0 - px + mx - py + my - 6.0 * diffusion
    coef = jnp.stack(
        [px + diffusion, diffusion - mx, py + diffusion, diffusion - my, base, base - settling,
         weight, jnp.float32(0.0)]
    ).astype(jnp.float32)
    r_lo, r_hi, lanes = ghost_pieces(src, obstacle)
    rows = nx + 2 * PAD
    width = ny + EXTRA
    any_spec = pl.BlockSpec(memory_space=pl.ANY)
    weighted = pl.pallas_call(
        make_kernel(nz, nx, ny, RZ),
        out_shape=jax.ShapeDtypeStruct((RZ, nx, ny), jnp.float32),
        in_specs=[pl.BlockSpec(memory_space=pltpu.SMEM)] + [any_spec] * 5,
        out_specs=pl.BlockSpec(memory_space=pltpu.VMEM),
        scratch_shapes=[
            pltpu.VMEM((nz, rows, width), jnp.float32),
            pltpu.VMEM((nz, rows, width), jnp.float32),
            pltpu.VMEM((nz, rows, width), jnp.float32),
            pltpu.VMEM((nz, nx, ny), jnp.int32),
            pltpu.SemaphoreType.DMA((8,)),
            pltpu.VMEM((rows, width), jnp.float32),
            pltpu.VMEM((rows, width), jnp.float32),
        ],
        compiler_params=pltpu.CompilerParams(vmem_limit_bytes=62 * 1024 * 1024),
    )(coef, source, obstacle, r_lo, r_hi, lanes)
    count = lax.axis_size("scen")
    parts = weighted.reshape(count, RZ // count, nx, ny)
    return lax.all_to_all(parts, "scen", 0, 0, tiled=True).sum(0)


def solution(mesh):
    in_specs = (P("scen", None, "gx", "gy"), P(None, "gx", "gy"), P("scen"), P("scen"))
    out_specs = P("scen", "gx", "gy")
    return jax.shard_map(
        on_device, mesh=mesh, in_specs=in_specs, out_specs=out_specs, check_vma=False
    )
```

```python
import math

import jax
import jax.numpy as jnp
from jax import lax
from jax.experimental import pallas as pl
from jax.experimental.pallas import tpu as pltpu
from jax.sharding import PartitionSpec as P

STEPS = 4
RZ = 16


wind_speed = 0.4
diffusion = 0.05
settling = 0.1
probit_a = 3.0
probit_b = 1.0
load_eps = 0.01
freq_rate = 0.7

H = STEPS
PAD = 16
EXTRA = 128
RB = 8
ROT_UNROLL = 34
ACC_UNROLL = 32
PLAIN_UNROLL = 34


def wind_components(sector_id):
    heading = sector_id.astype(jnp.float32) * (2.0 * math.pi / 16.0)
    return (wind_speed * jnp.cos(heading), wind_speed * jnp.sin(heading))


def _open_and_c(src, obs):
    open_cells = (1 - obs).astype(jnp.float32)
    return jnp.stack([src * open_cells, open_cells])


def _select(count, width, picks):
    cols = jnp.asarray(picks, jnp.int32)[:, None]
    return (lax.broadcasted_iota(jnp.int32, (count, width), 1) == cols).astype(jnp.float32)


def ghost_pieces(src, obs):
    nz, nx, ny = src.shape
    gxn = lax.axis_size("gx")
    gyn = lax.axis_size("gy")
    fx = [(i, i + 1) for i in range(gxn - 1)]
    bx = [(i + 1, i) for i in range(gxn - 1)]
    fy = [(i, i + 1) for i in range(gyn - 1)]
    by = [(i + 1, i) for i in range(gyn - 1)]
    hi = lax.Precision.HIGHEST
    last_rows = _open_and_c(src[:, nx - H:, :], obs[:, nx - H:, :])
    first_rows = _open_and_c(src[:, :H, :], obs[:, :H, :])
    xlo = lax.ppermute(last_rows, "gx", fx)
    xhi = lax.ppermute(first_rows, "gx", bx)
    pick = _select(2 * H, ny, list(range(H)) + list(range(ny - H, ny)))
    src_cols = jnp.einsum("zxy,ky->zkx", src, pick, precision=hi)
    open_cols = jnp.einsum("zxy,ky->zkx", (1 - obs).astype(jnp.float32), pick, precision=hi)
    cols = jnp.stack([src_cols * open_cols, open_cols])
    corner_lo = jnp.swapaxes(jnp.concatenate([xlo[..., :H], xlo[..., ny - H:]], -1), -1, -2)
    corner_hi = jnp.swapaxes(jnp.concatenate([xhi[..., :H], xhi[..., ny - H:]], -1), -1, -2)
    ext = jnp.concatenate([corner_lo, cols, corner_hi], axis=-1)
    yw = lax.ppermute(ext[:, :, H:], "gy", fy)
    ye = lax.ppermute(ext[:, :, :H], "gy", by)
    rows = nx + 2 * PAD
    yt = jnp.concatenate([ye, yw], axis=2)
    yt = jnp.pad(yt, ((0, 0), (0, 0), (0, 0), (PAD - H, rows - nx - PAD - H)))
    place = _select(2 * H, EXTRA, list(range(H)) + list(range(EXTRA - H, EXTRA)))
    lanes = jnp.einsum("czkr,kj->czrj", yt, place, precision=hi)
    r_lo = jnp.pad(xlo, ((0, 0), (0, 0), (PAD - H, 0), (0, 0)))
    r_hi = jnp.pad(xhi, ((0, 0), (0, 0), (0, PAD - H), (0, 0)))
    return r_lo, r_hi, lanes


def make_kernel(nz, nx, ny, rz):
    rows = nx + 2 * PAD
    width = ny + EXTRA
    nblk = rows // RB
    b_first = 1
    b_last = nblk - 2
    acc_lo = PAD // RB
    acc_hi = (PAD + nx) // RB

    def kernel(coef, src_hbm, obs_hbm, rlo_hbm, rhi_hbm, lanes_hbm, out_ref,
               a_buf, b_buf, o_buf, obs_buf, sems, s_buf, n_buf):
        copies = [
            pltpu.make_async_copy(obs_hbm, obs_buf, sems.at[0]),
            pltpu.make_async_copy(rlo_hbm.at[1], o_buf.at[:, pl.ds(0, PAD), pl.ds(0, ny)], sems.at[1]),
            pltpu.make_async_copy(rhi_hbm.at[1], o_buf.at[:, pl.ds(PAD + nx, PAD), pl.ds(0, ny)], sems.at[2]),
            pltpu.make_async_copy(lanes_hbm.at[1], o_buf.at[:, :, pl.ds(ny, EXTRA)], sems.at[3]),
            pltpu.make_async_copy(src_hbm.at[0], a_buf.at[:, pl.ds(PAD, nx), pl.ds(0, ny)], sems.at[4]),
            pltpu.make_async_copy(rlo_hbm.at[0], a_buf.at[:, pl.ds(0, PAD), pl.ds(0, ny)], sems.at[5]),
            pltpu.make_async_copy(rhi_hbm.at[0], a_buf.at[:, pl.ds(PAD + nx, PAD), pl.ds(0, ny)], sems.at[6]),
            pltpu.make_async_copy(lanes_hbm.at[0], a_buf.at[:, :, pl.ds(ny, EXTRA)], sems.at[7]),
        ]
        for cp in copies:
            cp.start()

        zeros = jnp.zeros((RB, width), jnp.float32)

        def clear(z, c):
            b_buf[z, pl.ds(0, RB), :] = zeros
            b_buf[z, pl.ds(rows - RB, RB), :] = zeros
            return c

        lax.fori_loop(0, nz, clear, 0)

        copies[0].wait()

        def to_open(z, c):
            o_buf[z, pl.ds(PAD, nx), pl.ds(0, ny)] = (1 - obs_buf[z]).astype(jnp.float32)
            return c

        lax.fori_loop(0, nz, to_open, 0)
        copies[4].wait()

        def to_c0(z, c):
            a_buf[z, pl.ds(PAD, nx), pl.ds(0, ny)] = (
                a_buf[z, pl.ds(PAD, nx), pl.ds(0, ny)] * o_buf[z, pl.ds(PAD, nx), pl.ds(0, ny)]
            )
            return c

        lax.fori_loop(0, nz, to_c0, 0)
        for cp in copies[1:4] + copies[5:]:
            cp.wait()

        k_w = coef[0]
        k_e = coef[1]
        k_s = coef[2]
        k_n = coef[3]
        k0_first = coef[4]
        k0_rest = coef[5]
        weight = coef[6]
        npc = width // 128
        nacc = ny // 128
        row_id = lax.broadcasted_iota(jnp.int32, (RB, 128), 0)
        lane_id = lax.broadcasted_iota(jnp.int32, (RB, 128), 1)
        first_row = row_id == 0
        last_row = row_id == RB - 1
        first_lane = lane_id == 0
        last_lane = lane_id == 127

        def pieces(ref, z, r):
            return tuple(ref[z, pl.ds(r, RB), pl.ds(128 * k, 128)] for k in range(npc))

        def step(src, dst, first):
            def level(z, accumulate):
                zu = jnp.minimum(z + 1, nz - 1)
                zl = jnp.maximum(z - 1, 0)
                k0 = jnp.where(z == 0, k0_first, k0_rest)
                ku = jnp.where(z == nz - 1, 0.0, diffusion + settling).astype(jnp.float32)

                def rot(b, c):
                    r = pl.multiple_of(b * RB, RB)
                    cur = pieces(src, z, r)
                    right = tuple(pltpu.roll(v, 1, 1) for v in cur)
                    left = tuple(pltpu.roll(v, 127, 1) for v in cur)
                    for k in range(npc):
                        s_buf[pl.ds(r, RB), pl.ds(128 * k, 128)] = jnp.where(
                            first_lane, right[(k - 1) % npc], right[k])
                        n_buf[pl.ds(r, RB), pl.ds(128 * k, 128)] = jnp.where(
                            last_lane, left[(k + 1) % npc], left[k])
                    return c

                lax.fori_loop(b_first, b_last + 1, rot, 0, unroll=ROT_UNROLL)

                def blk(b, carry, acc):
                    prev, cur = carry
                    r = pl.multiple_of(b * RB, RB)
                    nxt = pieces(src, z, r + RB)
                    up = pieces(src, zu, r)
                    low = pieces(src, zl, r)
                    o = pieces(o_buf, z, r)
                    ro = pl.multiple_of(r - PAD, RB)
                    for k in range(npc):
                        c = cur[k]
                        west = jnp.where(first_row, pltpu.roll(prev[k], 1, 0), pltpu.roll(c, 1, 0))
                        east = jnp.where(last_row, pltpu.roll(nxt[k], RB - 1, 0), pltpu.roll(c, RB - 1, 0))
                        south = s_buf[pl.ds(r, RB), pl.ds(128 * k, 128)]
                        north = n_buf[pl.ds(r, RB), pl.ds(128 * k, 128)]
                        new = o[k] * (
                            (k0 * c + k_w * west)
                            + (k_e * east + k_s * south)
                            + ((k_n * north + ku * up[k]) + diffusion * low[k])
                        )
                        dst[z, pl.ds(r, RB), pl.ds(128 * k, 128)] = new
                        if acc and k < nacc:
                            sq = new * new
                            if first:
                                out_ref[z, pl.ds(ro, RB), pl.ds(128 * k, 128)] = sq
                            else:
                                out_ref[z, pl.ds(ro, RB), pl.ds(128 * k, 128)] = (
                                    out_ref[z, pl.ds(ro, RB), pl.ds(128 * k, 128)] + sq
                                )
                    return (cur, nxt)

                carry = (pieces(src, z, 0), pieces(src, z, RB))
                if accumulate:
                    carry = lax.fori_loop(b_first, acc_lo, lambda b, c: blk(b, c, False), carry)
                    carry = lax.fori_loop(acc_lo, acc_hi, lambda b, c: blk(b, c, True), carry, unroll=ACC_UNROLL)
                    carry = lax.fori_loop(acc_hi, b_last + 1, lambda b, c: blk(b, c, False), carry)
                else:
                    carry = lax.fori_loop(b_first, b_last + 1, lambda b, c: blk(b, c, False), carry, unroll=PLAIN_UNROLL)

            def lvl_acc(z, c):
                level(z, True)
                return c

            def lvl_plain(z, c):
                level(z, False)
                return c

            lax.fori_loop(0, rz, lvl_acc, 0)
            lax.fori_loop(rz, nz, lvl_plain, 0)

        bufs = (a_buf, b_buf)
        for n in range(STEPS):
            step(bufs[n % 2], bufs[(n + 1) % 2], n == 0)

        def leth(z, c):
            for q in range(nx // 32):
                load = out_ref[z, pl.ds(q * 32, 32), :]
                probit = probit_a + probit_b * jnp.log(load + load_eps)
                lethal = 0.5 * (1.0 + lax.erf((probit - 5.0) / math.sqrt(2.0)))
                out_ref[z, pl.ds(q * 32, 32), :] = weight * lethal
            return c

        lax.fori_loop(0, rz, leth, 0)

    return kernel


def on_device(source, obstacle, sector, freq_class):
    src = source[0]
    nz, nx, ny = src.shape
    courant_x, courant_y = wind_components(sector[0])
    weight = jnp.exp(-freq_rate * freq_class[0].astype(jnp.float32))
    px = jnp.maximum(courant_x, 0.0)
    mx = jnp.minimum(courant_x, 0.0)
    py = jnp.maximum(courant_y, 0.0)
    my = jnp.minimum(courant_y, 0.0)
    base = 1.0 - px + mx - py + my - 6.0 * diffusion
    coef = jnp.stack(
        [px + diffusion, diffusion - mx, py + diffusion, diffusion - my, base, base - settling,
         weight, jnp.float32(0.0)]
    ).astype(jnp.float32)
    r_lo, r_hi, lanes = ghost_pieces(src, obstacle)
    rows = nx + 2 * PAD
    width = ny + EXTRA
    any_spec = pl.BlockSpec(memory_space=pl.ANY)
    weighted = pl.pallas_call(
        make_kernel(nz, nx, ny, RZ),
        out_shape=jax.ShapeDtypeStruct((RZ, nx, ny), jnp.float32),
        in_specs=[pl.BlockSpec(memory_space=pltpu.SMEM)] + [any_spec] * 5,
        out_specs=pl.BlockSpec(memory_space=pltpu.VMEM),
        scratch_shapes=[
            pltpu.VMEM((nz, rows, width), jnp.float32),
            pltpu.VMEM((nz, rows, width), jnp.float32),
            pltpu.VMEM((nz, rows, width), jnp.float32),
            pltpu.VMEM((nz, nx, ny), jnp.int32),
            pltpu.SemaphoreType.DMA((8,)),
            pltpu.VMEM((rows, width), jnp.float32),
            pltpu.VMEM((rows, width), jnp.float32),
        ],
        compiler_params=pltpu.CompilerParams(vmem_limit_bytes=62 * 1024 * 1024),
    )(coef, source, obstacle, r_lo, r_hi, lanes)
    count = lax.axis_size("scen")
    parts = weighted.reshape(count, RZ // count, nx, ny)
    return lax.all_to_all(parts, "scen", 0, 0, tiled=True).sum(0)


def solution(mesh):
    in_specs = (P("scen", None, "gx", "gy"), P(None, "gx", "gy"), P("scen"), P("scen"))
    out_specs = P("scen", "gx", "gy")
    return jax.shard_map(
        on_device, mesh=mesh, in_specs=in_specs, out_specs=out_specs, check_vma=False
    )
```

```python
import math

import jax
import jax.numpy as jnp
from jax import lax
from jax.experimental import pallas as pl
from jax.experimental.pallas import tpu as pltpu
from jax.sharding import PartitionSpec as P

STEPS = 4
RZ = 16


wind_speed = 0.4
diffusion = 0.05
settling = 0.1
probit_a = 3.0
probit_b = 1.0
load_eps = 0.01
freq_rate = 0.7

H = STEPS
PAD = 16
EXTRA = 128
RB = 8
ROT_UNROLL = 34
ACC_UNROLL = 32
PLAIN_UNROLL = 34


def wind_components(sector_id):
    heading = sector_id.astype(jnp.float32) * (2.0 * math.pi / 16.0)
    return (wind_speed * jnp.cos(heading), wind_speed * jnp.sin(heading))


def _open_and_c(src, obs):
    open_cells = (1 - obs).astype(jnp.float32)
    return jnp.stack([src * open_cells, open_cells])


def _select(count, width, picks):
    cols = jnp.asarray(picks, jnp.int32)[:, None]
    return (lax.broadcasted_iota(jnp.int32, (count, width), 1) == cols).astype(jnp.float32)


def ghost_pieces(src, obs):
    nz, nx, ny = src.shape
    gxn = lax.axis_size("gx")
    gyn = lax.axis_size("gy")
    fx = [(i, i + 1) for i in range(gxn - 1)]
    bx = [(i + 1, i) for i in range(gxn - 1)]
    fy = [(i, i + 1) for i in range(gyn - 1)]
    by = [(i + 1, i) for i in range(gyn - 1)]
    hi = lax.Precision.HIGHEST
    last_rows = _open_and_c(src[:, nx - H:, :], obs[:, nx - H:, :])
    first_rows = _open_and_c(src[:, :H, :], obs[:, :H, :])
    xlo = lax.ppermute(last_rows, "gx", fx)
    xhi = lax.ppermute(first_rows, "gx", bx)
    pick = _select(2 * H, ny, list(range(H)) + list(range(ny - H, ny)))
    src_cols = jnp.einsum("zxy,ky->zkx", src, pick, precision=hi)
    open_cols = jnp.einsum("zxy,ky->zkx", (1 - obs).astype(jnp.float32), pick, precision=hi)
    cols = jnp.stack([src_cols * open_cols, open_cols])
    corner_lo = jnp.swapaxes(jnp.concatenate([xlo[..., :H], xlo[..., ny - H:]], -1), -1, -2)
    corner_hi = jnp.swapaxes(jnp.concatenate([xhi[..., :H], xhi[..., ny - H:]], -1), -1, -2)
    ext = jnp.concatenate([corner_lo, cols, corner_hi], axis=-1)
    yw = lax.ppermute(ext[:, :, H:], "gy", fy)
    ye = lax.ppermute(ext[:, :, :H], "gy", by)
    rows = nx + 2 * PAD
    yt = jnp.concatenate([ye, yw], axis=2)
    span = -(-rows // 128) * 128
    lanes = jnp.pad(yt, ((0, 0), (0, 0), (0, 0), (PAD - H, span - nx - PAD - H)))
    r_lo = jnp.pad(xlo, ((0, 0), (0, 0), (PAD - H, 0), (0, 0)))
    r_hi = jnp.pad(xhi, ((0, 0), (0, 0), (0, PAD - H), (0, 0)))
    return r_lo, r_hi, lanes


def make_kernel(nz, nx, ny, rz):
    rows = nx + 2 * PAD
    width = ny + EXTRA
    nblk = rows // RB
    b_first = 1
    b_last = nblk - 2
    acc_lo = PAD // RB
    acc_hi = (PAD + nx) // RB

    def kernel(coef, src_hbm, obs_hbm, rlo_hbm, rhi_hbm, lanes_ref, out_ref,
               a_buf, b_buf, o_buf, obs_buf, sems, s_buf, n_buf):
        copies = [
            pltpu.make_async_copy(obs_hbm, obs_buf, sems.at[0]),
            pltpu.make_async_copy(rlo_hbm.at[1], o_buf.at[:, pl.ds(0, PAD), pl.ds(0, ny)], sems.at[1]),
            pltpu.make_async_copy(rhi_hbm.at[1], o_buf.at[:, pl.ds(PAD + nx, PAD), pl.ds(0, ny)], sems.at[2]),
            pltpu.make_async_copy(src_hbm.at[0], a_buf.at[:, pl.ds(PAD, nx), pl.ds(0, ny)], sems.at[4]),
            pltpu.make_async_copy(rlo_hbm.at[0], a_buf.at[:, pl.ds(0, PAD), pl.ds(0, ny)], sems.at[5]),
            pltpu.make_async_copy(rhi_hbm.at[0], a_buf.at[:, pl.ds(PAD + nx, PAD), pl.ds(0, ny)], sems.at[6]),
        ]
        for cp in copies:
            cp.start()

        k_id = lax.broadcasted_iota(jnp.int32, (2 * H, EXTRA), 0)
        j_id = lax.broadcasted_iota(jnp.int32, (2 * H, EXTRA), 1)
        dest = jnp.where(k_id < H, k_id, k_id + EXTRA - 2 * H)
        place = (j_id == dest).astype(jnp.float32)

        def put_lanes(z, c):
            for buf, part in ((a_buf, 0), (o_buf, 1)):
                placed = lax.dot_general(
                    lanes_ref[part, z], place, (((0,), (0,)), ((), ())),
                    precision=lax.Precision.HIGHEST, preferred_element_type=jnp.float32)
                buf[z, :, pl.ds(ny, EXTRA)] = placed[:rows]
            return c

        lax.fori_loop(0, nz, put_lanes, 0)

        zeros = jnp.zeros((RB, width), jnp.float32)

        def clear(z, c):
            b_buf[z, pl.ds(0, RB), :] = zeros
            b_buf[z, pl.ds(rows - RB, RB), :] = zeros
            return c

        lax.fori_loop(0, nz, clear, 0)

        copies[0].wait()

        def to_open(z, c):
            o_buf[z, pl.ds(PAD, nx), pl.ds(0, ny)] = (1 - obs_buf[z]).astype(jnp.float32)
            return c

        lax.fori_loop(0, nz, to_open, 0)
        copies[3].wait()

        def to_c0(z, c):
            a_buf[z, pl.ds(PAD, nx), pl.ds(0, ny)] = (
                a_buf[z, pl.ds(PAD, nx), pl.ds(0, ny)] * o_buf[z, pl.ds(PAD, nx), pl.ds(0, ny)]
            )
            return c

        lax.fori_loop(0, nz, to_c0, 0)
        for cp in copies[1:3] + copies[4:]:
            cp.wait()

        k_w = coef[0]
        k_e = coef[1]
        k_s = coef[2]
        k_n = coef[3]
        k0_first = coef[4]
        k0_rest = coef[5]
        weight = coef[6]
        npc = width // 128
        nacc = ny // 128
        row_id = lax.broadcasted_iota(jnp.int32, (RB, 128), 0)
        lane_id = lax.broadcasted_iota(jnp.int32, (RB, 128), 1)
        first_row = row_id == 0
        last_row = row_id == RB - 1
        first_lane = lane_id == 0
        last_lane = lane_id == 127

        def pieces(ref, z, r):
            return tuple(ref[z, pl.ds(r, RB), pl.ds(128 * k, 128)] for k in range(npc))

        def step(src, dst, first):
            def level(z, accumulate):
                zu = jnp.minimum(z + 1, nz - 1)
                zl = jnp.maximum(z - 1, 0)
                k0 = jnp.where(z == 0, k0_first, k0_rest)
                ku = jnp.where(z == nz - 1, 0.0, diffusion + settling).astype(jnp.float32)

                def rot(b, c):
                    r = pl.multiple_of(b * RB, RB)
                    cur = pieces(src, z, r)
                    right = tuple(pltpu.roll(v, 1, 1) for v in cur)
                    left = tuple(pltpu.roll(v, 127, 1) for v in cur)
                    for k in range(npc):
                        s_buf[pl.ds(r, RB), pl.ds(128 * k, 128)] = jnp.where(
                            first_lane, right[(k - 1) % npc], right[k])
                        n_buf[pl.ds(r, RB), pl.ds(128 * k, 128)] = jnp.where(
                            last_lane, left[(k + 1) % npc], left[k])
                    return c

                lax.fori_loop(b_first, b_last + 1, rot, 0, unroll=ROT_UNROLL)

                def blk(b, carry, acc):
                    prev, cur = carry
                    r = pl.multiple_of(b * RB, RB)
                    nxt = pieces(src, z, r + RB)
                    up = pieces(src, zu, r)
                    low = pieces(src, zl, r)
                    o = pieces(o_buf, z, r)
                    ro = pl.multiple_of(r - PAD, RB)
                    for k in range(npc):
                        c = cur[k]
                        west = jnp.where(first_row, pltpu.roll(prev[k], 1, 0), pltpu.roll(c, 1, 0))
                        east = jnp.where(last_row, pltpu.roll(nxt[k], RB - 1, 0), pltpu.roll(c, RB - 1, 0))
                        south = s_buf[pl.ds(r, RB), pl.ds(128 * k, 128)]
                        north = n_buf[pl.ds(r, RB), pl.ds(128 * k, 128)]
                        new = o[k] * (
                            (k0 * c + k_w * west)
                            + (k_e * east + k_s * south)
                            + ((k_n * north + ku * up[k]) + diffusion * low[k])
                        )
                        dst[z, pl.ds(r, RB), pl.ds(128 * k, 128)] = new
                        if acc and k < nacc:
                            sq = new * new
                            if first:
                                out_ref[z, pl.ds(ro, RB), pl.ds(128 * k, 128)] = sq
                            else:
                                out_ref[z, pl.ds(ro, RB), pl.ds(128 * k, 128)] = (
                                    out_ref[z, pl.ds(ro, RB), pl.ds(128 * k, 128)] + sq
                                )
                    return (cur, nxt)

                carry = (pieces(src, z, 0), pieces(src, z, RB))
                if accumulate:
                    carry = lax.fori_loop(b_first, acc_lo, lambda b, c: blk(b, c, False), carry)
                    carry = lax.fori_loop(acc_lo, acc_hi, lambda b, c: blk(b, c, True), carry, unroll=ACC_UNROLL)
                    carry = lax.fori_loop(acc_hi, b_last + 1, lambda b, c: blk(b, c, False), carry)
                else:
                    carry = lax.fori_loop(b_first, b_last + 1, lambda b, c: blk(b, c, False), carry, unroll=PLAIN_UNROLL)

            def lvl_acc(z, c):
                level(z, True)
                return c

            def lvl_plain(z, c):
                level(z, False)
                return c

            lax.fori_loop(0, rz, lvl_acc, 0)
            lax.fori_loop(rz, nz, lvl_plain, 0)

        bufs = (a_buf, b_buf)
        for n in range(STEPS):
            step(bufs[n % 2], bufs[(n + 1) % 2], n == 0)

        def leth(z, c):
            for q in range(nx // 32):
                load = out_ref[z, pl.ds(q * 32, 32), :]
                probit = probit_a + probit_b * jnp.log(load + load_eps)
                lethal = 0.5 * (1.0 + lax.erf((probit - 5.0) / math.sqrt(2.0)))
                out_ref[z, pl.ds(q * 32, 32), :] = weight * lethal
            return c

        lax.fori_loop(0, rz, leth, 0)

    return kernel


def on_device(source, obstacle, sector, freq_class):
    src = source[0]
    nz, nx, ny = src.shape
    courant_x, courant_y = wind_components(sector[0])
    weight = jnp.exp(-freq_rate * freq_class[0].astype(jnp.float32))
    px = jnp.maximum(courant_x, 0.0)
    mx = jnp.minimum(courant_x, 0.0)
    py = jnp.maximum(courant_y, 0.0)
    my = jnp.minimum(courant_y, 0.0)
    base = 1.0 - px + mx - py + my - 6.0 * diffusion
    coef = jnp.stack(
        [px + diffusion, diffusion - mx, py + diffusion, diffusion - my, base, base - settling,
         weight, jnp.float32(0.0)]
    ).astype(jnp.float32)
    r_lo, r_hi, lanes = ghost_pieces(src, obstacle)
    rows = nx + 2 * PAD
    width = ny + EXTRA
    any_spec = pl.BlockSpec(memory_space=pl.ANY)
    weighted = pl.pallas_call(
        make_kernel(nz, nx, ny, RZ),
        out_shape=jax.ShapeDtypeStruct((RZ, nx, ny), jnp.float32),
        in_specs=[pl.BlockSpec(memory_space=pltpu.SMEM)] + [any_spec] * 4
        + [pl.BlockSpec(memory_space=pltpu.VMEM)],
        out_specs=pl.BlockSpec(memory_space=pltpu.VMEM),
        scratch_shapes=[
            pltpu.VMEM((nz, rows, width), jnp.float32),
            pltpu.VMEM((nz, rows, width), jnp.float32),
            pltpu.VMEM((nz, rows, width), jnp.float32),
            pltpu.VMEM((nz, nx, ny), jnp.int32),
            pltpu.SemaphoreType.DMA((8,)),
            pltpu.VMEM((rows, width), jnp.float32),
            pltpu.VMEM((rows, width), jnp.float32),
        ],
        compiler_params=pltpu.CompilerParams(vmem_limit_bytes=62 * 1024 * 1024),
    )(coef, source, obstacle, r_lo, r_hi, lanes)
    count = lax.axis_size("scen")
    parts = weighted.reshape(count, RZ // count, nx, ny)
    return lax.all_to_all(parts, "scen", 0, 0, tiled=True).sum(0)


def solution(mesh):
    in_specs = (P("scen", None, "gx", "gy"), P(None, "gx", "gy"), P("scen"), P("scen"))
    out_specs = P("scen", "gx", "gy")
    return jax.shard_map(
        on_device, mesh=mesh, in_specs=in_specs, out_specs=out_specs, check_vma=False
    )
```

```python
import math

import jax
import jax.numpy as jnp
from jax import lax
from jax.experimental import pallas as pl
from jax.experimental.pallas import tpu as pltpu
from jax.sharding import PartitionSpec as P

STEPS = 4
RZ = 16


wind_speed = 0.4
diffusion = 0.05
settling = 0.1
probit_a = 3.0
probit_b = 1.0
load_eps = 0.01
freq_rate = 0.7

H = STEPS
PAD = 16
EXTRA = 128
RB = 8


def wind_components(sector_id):
    heading = sector_id.astype(jnp.float32) * (2.0 * math.pi / 16.0)
    return (wind_speed * jnp.cos(heading), wind_speed * jnp.sin(heading))


def _open_and_c(src, obs):
    open_cells = (1 - obs).astype(jnp.float32)
    return jnp.stack([src * open_cells, open_cells])


def _select(count, width, picks):
    cols = jnp.asarray(picks, jnp.int32)[:, None]
    return (lax.broadcasted_iota(jnp.int32, (count, width), 1) == cols).astype(jnp.float32)


def ghost_pieces(src, obs):
    nz, nx, ny = src.shape
    gxn = lax.axis_size("gx")
    gyn = lax.axis_size("gy")
    fx = [(i, i + 1) for i in range(gxn - 1)]
    bx = [(i + 1, i) for i in range(gxn - 1)]
    fy = [(i, i + 1) for i in range(gyn - 1)]
    by = [(i + 1, i) for i in range(gyn - 1)]
    hi = lax.Precision.HIGHEST
    last_rows = _open_and_c(src[:, nx - H:, :], obs[:, nx - H:, :])
    first_rows = _open_and_c(src[:, :H, :], obs[:, :H, :])
    xlo = lax.ppermute(last_rows, "gx", fx)
    xhi = lax.ppermute(first_rows, "gx", bx)
    pick = _select(2 * H, ny, list(range(H)) + list(range(ny - H, ny)))
    src_cols = jnp.einsum("zxy,ky->zkx", src, pick, precision=hi)
    open_cols = jnp.einsum("zxy,ky->zkx", (1 - obs).astype(jnp.float32), pick, precision=hi)
    cols = jnp.stack([src_cols * open_cols, open_cols])
    corner_lo = jnp.swapaxes(jnp.concatenate([xlo[..., :H], xlo[..., ny - H:]], -1), -1, -2)
    corner_hi = jnp.swapaxes(jnp.concatenate([xhi[..., :H], xhi[..., ny - H:]], -1), -1, -2)
    ext = jnp.concatenate([corner_lo, cols, corner_hi], axis=-1)
    yw = lax.ppermute(ext[:, :, H:], "gy", fy)
    ye = lax.ppermute(ext[:, :, :H], "gy", by)
    rows = nx + 2 * PAD
    yt = jnp.concatenate([ye, yw], axis=2)
    yt = jnp.pad(yt, ((0, 0), (0, 0), (0, 0), (PAD - H, rows - nx - PAD - H)))
    place = _select(2 * H, EXTRA, list(range(H)) + list(range(EXTRA - H, EXTRA)))
    lanes = jnp.einsum("czkr,kj->czrj", yt, place, precision=hi)
    r_lo = jnp.pad(xlo, ((0, 0), (0, 0), (PAD - H, 0), (0, 0)))
    r_hi = jnp.pad(xhi, ((0, 0), (0, 0), (0, PAD - H), (0, 0)))
    return r_lo, r_hi, lanes


def make_kernel(nz, nx, ny, rz, half):
    nh = nx // 2
    rows = nh + 2 * PAD
    width = ny + EXTRA
    nblk = rows // RB
    b_first = 1
    b_last = nblk - 2
    acc_lo = PAD // RB
    acc_hi = (PAD + nh) // RB
    nb = nh + PAD
    s0 = 0 if half == 0 else nx - nb
    b0 = PAD if half == 0 else 0
    g0 = 0 if half == 0 else nb
    lane0 = 0 if half == 0 else nh

    def kernel(coef, src_hbm, obs_hbm, ghost_hbm, lanes_hbm, out_ref,
               a_buf, b_buf, o_buf, obs_buf, sems, s_buf, n_buf):
        copies = [
            pltpu.make_async_copy(obs_hbm.at[:, pl.ds(s0, nb), :], obs_buf, sems.at[0]),
            pltpu.make_async_copy(ghost_hbm.at[1], o_buf.at[:, pl.ds(g0, PAD), pl.ds(0, ny)], sems.at[1]),
            pltpu.make_async_copy(lanes_hbm.at[1, :, pl.ds(lane0, rows)], o_buf.at[:, :, pl.ds(ny, EXTRA)], sems.at[3]),
            pltpu.make_async_copy(src_hbm.at[0, :, pl.ds(s0, nb), :], a_buf.at[:, pl.ds(b0, nb), pl.ds(0, ny)], sems.at[4]),
            pltpu.make_async_copy(ghost_hbm.at[0], a_buf.at[:, pl.ds(g0, PAD), pl.ds(0, ny)], sems.at[5]),
            pltpu.make_async_copy(lanes_hbm.at[0, :, pl.ds(lane0, rows)], a_buf.at[:, :, pl.ds(ny, EXTRA)], sems.at[7]),
        ]
        for cp in copies:
            cp.start()

        zeros = jnp.zeros((RB, width), jnp.float32)

        def clear(z, c):
            b_buf[z, pl.ds(0, RB), :] = zeros
            b_buf[z, pl.ds(rows - RB, RB), :] = zeros
            return c

        lax.fori_loop(0, nz, clear, 0)

        copies[0].wait()

        def to_open(z, c):
            o_buf[z, pl.ds(b0, nb), pl.ds(0, ny)] = (1 - obs_buf[z]).astype(jnp.float32)
            return c

        lax.fori_loop(0, nz, to_open, 0)
        copies[3].wait()

        def to_c0(z, c):
            a_buf[z, pl.ds(b0, nb), pl.ds(0, ny)] = (
                a_buf[z, pl.ds(b0, nb), pl.ds(0, ny)] * o_buf[z, pl.ds(b0, nb), pl.ds(0, ny)]
            )
            return c

        lax.fori_loop(0, nz, to_c0, 0)
        for cp in copies[1:3] + copies[4:]:
            cp.wait()

        k_w = coef[0]
        k_e = coef[1]
        k_s = coef[2]
        k_n = coef[3]
        k0_first = coef[4]
        k0_rest = coef[5]
        weight = coef[6]
        npc = width // 128
        nacc = ny // 128
        row_id = lax.broadcasted_iota(jnp.int32, (RB, 128), 0)
        lane_id = lax.broadcasted_iota(jnp.int32, (RB, 128), 1)
        first_row = row_id == 0
        last_row = row_id == RB - 1
        first_lane = lane_id == 0
        last_lane = lane_id == 127

        def pieces(ref, z, r):
            return tuple(ref[z, pl.ds(r, RB), pl.ds(128 * k, 128)] for k in range(npc))

        def step(src, dst, first):
            def level(z, accumulate):
                zu = jnp.minimum(z + 1, nz - 1)
                zl = jnp.maximum(z - 1, 0)
                k0 = jnp.where(z == 0, k0_first, k0_rest)
                ku = jnp.where(z == nz - 1, 0.0, diffusion + settling).astype(jnp.float32)

                def rot(b, c):
                    r = pl.multiple_of(b * RB, RB)
                    cur = pieces(src, z, r)
                    right = tuple(pltpu.roll(v, 1, 1) for v in cur)
                    left = tuple(pltpu.roll(v, 127, 1) for v in cur)
                    for k in range(npc):
                        s_buf[pl.ds(r, RB), pl.ds(128 * k, 128)] = jnp.where(
                            first_lane, right[(k - 1) % npc], right[k])
                        n_buf[pl.ds(r, RB), pl.ds(128 * k, 128)] = jnp.where(
                            last_lane, left[(k + 1) % npc], left[k])
                    return c

                lax.fori_loop(b_first, b_last + 1, rot, 0, unroll=True)

                def blk(b, carry, acc):
                    prev, cur = carry
                    r = pl.multiple_of(b * RB, RB)
                    nxt = pieces(src, z, r + RB)
                    up = pieces(src, zu, r)
                    low = pieces(src, zl, r)
                    o = pieces(o_buf, z, r)
                    ro = pl.multiple_of(r - PAD, RB)
                    for k in range(npc):
                        c = cur[k]
                        west = jnp.where(first_row, pltpu.roll(prev[k], 1, 0), pltpu.roll(c, 1, 0))
                        east = jnp.where(last_row, pltpu.roll(nxt[k], RB - 1, 0), pltpu.roll(c, RB - 1, 0))
                        south = s_buf[pl.ds(r, RB), pl.ds(128 * k, 128)]
                        north = n_buf[pl.ds(r, RB), pl.ds(128 * k, 128)]
                        new = o[k] * (
                            (k0 * c + k_w * west)
                            + (k_e * east + k_s * south)
                            + ((k_n * north + ku * up[k]) + diffusion * low[k])
                        )
                        dst[z, pl.ds(r, RB), pl.ds(128 * k, 128)] = new
                        if acc and k < nacc:
                            sq = new * new
                            if first:
                                out_ref[z, pl.ds(ro, RB), pl.ds(128 * k, 128)] = sq
                            else:
                                out_ref[z, pl.ds(ro, RB), pl.ds(128 * k, 128)] = (
                                    out_ref[z, pl.ds(ro, RB), pl.ds(128 * k, 128)] + sq
                                )
                    return (cur, nxt)

                carry = (pieces(src, z, 0), pieces(src, z, RB))
                if accumulate:
                    carry = lax.fori_loop(b_first, acc_lo, lambda b, c: blk(b, c, False), carry)
                    carry = lax.fori_loop(acc_lo, acc_hi, lambda b, c: blk(b, c, True), carry, unroll=True)
                    carry = lax.fori_loop(acc_hi, b_last + 1, lambda b, c: blk(b, c, False), carry)
                else:
                    carry = lax.fori_loop(b_first, b_last + 1, lambda b, c: blk(b, c, False), carry, unroll=True)

            def lvl_acc(z, c):
                level(z, True)
                return c

            def lvl_plain(z, c):
                level(z, False)
                return c

            lax.fori_loop(0, rz, lvl_acc, 0)
            lax.fori_loop(rz, nz, lvl_plain, 0)

        bufs = (a_buf, b_buf)
        for n in range(STEPS):
            step(bufs[n % 2], bufs[(n + 1) % 2], n == 0)

        def leth(z, c):
            for q in range(nh // 32):
                load = out_ref[z, pl.ds(q * 32, 32), :]
                probit = probit_a + probit_b * jnp.log(load + load_eps)
                lethal = 0.5 * (1.0 + lax.erf((probit - 5.0) / math.sqrt(2.0)))
                out_ref[z, pl.ds(q * 32, 32), :] = weight * lethal
            return c

        lax.fori_loop(0, rz, leth, 0)

    return kernel


def _reduce_sync(weighted):
    count = lax.axis_size("scen")
    parts = weighted.reshape((count, RZ // count) + weighted.shape[1:])
    return lax.all_to_all(parts, "scen", 0, 0, tiled=True).sum(0)


def on_device(source, obstacle, sector, freq_class):
    src = source[0]
    nz, nx, ny = src.shape
    courant_x, courant_y = wind_components(sector[0])
    weight = jnp.exp(-freq_rate * freq_class[0].astype(jnp.float32))
    px = jnp.maximum(courant_x, 0.0)
    mx = jnp.minimum(courant_x, 0.0)
    py = jnp.maximum(courant_y, 0.0)
    my = jnp.minimum(courant_y, 0.0)
    base = 1.0 - px + mx - py + my - 6.0 * diffusion
    coef = jnp.stack(
        [px + diffusion, diffusion - mx, py + diffusion, diffusion - my, base, base - settling,
         weight, jnp.float32(0.0)]
    ).astype(jnp.float32)
    r_lo, r_hi, lanes = ghost_pieces(src, obstacle)
    nh = nx // 2
    rows = nh + 2 * PAD
    width = ny + EXTRA
    any_spec = pl.BlockSpec(memory_space=pl.ANY)
    halves = []
    for half, ghost in ((0, r_lo), (1, r_hi)):
        halves.append(pl.pallas_call(
            make_kernel(nz, nx, ny, RZ, half),
            out_shape=jax.ShapeDtypeStruct((RZ, nh, ny), jnp.float32),
            in_specs=[pl.BlockSpec(memory_space=pltpu.SMEM)] + [any_spec] * 4,
            out_specs=pl.BlockSpec(memory_space=pltpu.VMEM),
            scratch_shapes=[
                pltpu.VMEM((nz, rows, width), jnp.float32),
                pltpu.VMEM((nz, rows, width), jnp.float32),
                pltpu.VMEM((nz, rows, width), jnp.float32),
                pltpu.VMEM((nz, nh + PAD, ny), jnp.int32),
                pltpu.SemaphoreType.DMA((8,)),
                pltpu.VMEM((rows, width), jnp.float32),
                pltpu.VMEM((rows, width), jnp.float32),
            ],
            compiler_params=pltpu.CompilerParams(vmem_limit_bytes=62 * 1024 * 1024),
        )(coef, source, obstacle, ghost, lanes))
        if half == 0:
            first = _reduce_sync(halves[0])
    second = _reduce_sync(halves[1])
    return jnp.concatenate([first, second], axis=1)


def solution(mesh):
    in_specs = (P("scen", None, "gx", "gy"), P(None, "gx", "gy"), P("scen"), P("scen"))
    out_specs = P("scen", "gx", "gy")
    return jax.shard_map(
        on_device, mesh=mesh, in_specs=in_specs, out_specs=out_specs, check_vma=False
    )
```

```python
import math

import jax
import jax.numpy as jnp
from jax import lax
from jax.experimental import pallas as pl
from jax.experimental.pallas import tpu as pltpu
from jax.sharding import PartitionSpec as P

STEPS = 4
RZ = 16


wind_speed = 0.4
diffusion = 0.05
settling = 0.1
probit_a = 3.0
probit_b = 1.0
load_eps = 0.01
freq_rate = 0.7

H = STEPS
PAD = 16
EXTRA = 128
RB = 8


def wind_components(sector_id):
    heading = sector_id.astype(jnp.float32) * (2.0 * math.pi / 16.0)
    return (wind_speed * jnp.cos(heading), wind_speed * jnp.sin(heading))


def _open_and_c(src, obs):
    open_cells = (1 - obs).astype(jnp.float32)
    return jnp.stack([src * open_cells, open_cells])


def _select(count, width, picks):
    cols = jnp.asarray(picks, jnp.int32)[:, None]
    return (lax.broadcasted_iota(jnp.int32, (count, width), 1) == cols).astype(jnp.float32)


def _split3(x):
    def bf(v):
        return lax.reduce_precision(v, exponent_bits=8, mantissa_bits=7)

    top = bf(x)
    rest = x - top
    mid = bf(rest)
    low = rest - mid
    return (top.astype(jnp.bfloat16), mid.astype(jnp.bfloat16), low.astype(jnp.bfloat16))


def ghost_pieces(src, obs):
    nz, nx, ny = src.shape
    gxn = lax.axis_size("gx")
    gyn = lax.axis_size("gy")
    fx = [(i, i + 1) for i in range(gxn - 1)]
    bx = [(i + 1, i) for i in range(gxn - 1)]
    fy = [(i, i + 1) for i in range(gyn - 1)]
    by = [(i + 1, i) for i in range(gyn - 1)]
    hi = lax.Precision.HIGHEST
    last_rows = _open_and_c(src[:, nx - H:, :], obs[:, nx - H:, :])
    first_rows = _open_and_c(src[:, :H, :], obs[:, :H, :])
    xlo = lax.ppermute(last_rows, "gx", fx)
    xhi = lax.ppermute(first_rows, "gx", bx)
    pick = _select(2 * H, ny, list(range(H)) + list(range(ny - H, ny)))
    src_cols = jnp.einsum("zxy,ky->zkx", src, pick, precision=hi)
    open_cols = jnp.einsum(
        "zxy,ky->zkx", (1 - obs).astype(jnp.bfloat16), pick.astype(jnp.bfloat16),
        preferred_element_type=jnp.float32)
    cols = jnp.stack([src_cols * open_cols, open_cols])
    corner_lo = jnp.swapaxes(jnp.concatenate([xlo[..., :H], xlo[..., ny - H:]], -1), -1, -2)
    corner_hi = jnp.swapaxes(jnp.concatenate([xhi[..., :H], xhi[..., ny - H:]], -1), -1, -2)
    ext = jnp.concatenate([corner_lo, cols, corner_hi], axis=-1)
    yw = lax.ppermute(ext[:, :, H:], "gy", fy)
    ye = lax.ppermute(ext[:, :, :H], "gy", by)
    rows = nx + 2 * PAD
    yt = jnp.concatenate([ye, yw], axis=2)
    yt = jnp.pad(yt, ((0, 0), (0, 0), (0, 0), (PAD - H, rows - nx - PAD - H)))
    place = _select(2 * H, EXTRA, list(range(H)) + list(range(EXTRA - H, EXTRA)))
    place = jnp.concatenate([place] * 3, 0).astype(jnp.bfloat16)
    lanes = jnp.einsum(
        "czkr,kj->czrj", jnp.concatenate(_split3(yt), 2), place,
        preferred_element_type=jnp.float32)
    r_lo = jnp.pad(xlo, ((0, 0), (0, 0), (PAD - H, 0), (0, 0)))
    r_hi = jnp.pad(xhi, ((0, 0), (0, 0), (0, PAD - H), (0, 0)))
    return r_lo, r_hi, lanes


def make_kernel(nz, nx, ny, rz, half):
    nh = nx // 2
    rows = nh + 2 * PAD
    width = ny + EXTRA
    nblk = rows // RB
    b_first = 1
    b_last = nblk - 2
    acc_lo = PAD // RB
    acc_hi = (PAD + nh) // RB
    nb = nh + PAD
    s0 = 0 if half == 0 else nx - nb
    b0 = PAD if half == 0 else 0
    g0 = 0 if half == 0 else nb
    lane0 = 0 if half == 0 else nh

    def kernel(coef, src_hbm, obs_hbm, ghost_hbm, lanes_hbm, out_ref,
               a_buf, b_buf, o_buf, obs_buf, sems, s_buf, n_buf):
        copies = [
            pltpu.make_async_copy(obs_hbm.at[:, pl.ds(s0, nb), :], obs_buf, sems.at[0]),
            pltpu.make_async_copy(ghost_hbm.at[1], o_buf.at[:, pl.ds(g0, PAD), pl.ds(0, ny)], sems.at[1]),
            pltpu.make_async_copy(lanes_hbm.at[1, :, pl.ds(lane0, rows)], o_buf.at[:, :, pl.ds(ny, EXTRA)], sems.at[3]),
            pltpu.make_async_copy(src_hbm.at[0, :, pl.ds(s0, nb), :], a_buf.at[:, pl.ds(b0, nb), pl.ds(0, ny)], sems.at[4]),
            pltpu.make_async_copy(ghost_hbm.at[0], a_buf.at[:, pl.ds(g0, PAD), pl.ds(0, ny)], sems.at[5]),
            pltpu.make_async_copy(lanes_hbm.at[0, :, pl.ds(lane0, rows)], a_buf.at[:, :, pl.ds(ny, EXTRA)], sems.at[7]),
        ]
        for cp in copies:
            cp.start()

        zeros = jnp.zeros((RB, width), jnp.float32)

        def clear(z, c):
            b_buf[z, pl.ds(0, RB), :] = zeros
            b_buf[z, pl.ds(rows - RB, RB), :] = zeros
            return c

        lax.fori_loop(0, nz, clear, 0)

        copies[0].wait()

        def to_open(z, c):
            o_buf[z, pl.ds(b0, nb), pl.ds(0, ny)] = (1 - obs_buf[z]).astype(jnp.float32)
            return c

        lax.fori_loop(0, nz, to_open, 0)
        copies[3].wait()

        def to_c0(z, c):
            a_buf[z, pl.ds(b0, nb), pl.ds(0, ny)] = (
                a_buf[z, pl.ds(b0, nb), pl.ds(0, ny)] * o_buf[z, pl.ds(b0, nb), pl.ds(0, ny)]
            )
            return c

        lax.fori_loop(0, nz, to_c0, 0)
        for cp in copies[1:3] + copies[4:]:
            cp.wait()

        k_w = coef[0]
        k_e = coef[1]
        k_s = coef[2]
        k_n = coef[3]
        k0_first = coef[4]
        k0_rest = coef[5]
        weight = coef[6]
        npc = width // 128
        nacc = ny // 128
        row_id = lax.broadcasted_iota(jnp.int32, (RB, 128), 0)
        lane_id = lax.broadcasted_iota(jnp.int32, (RB, 128), 1)
        first_row = row_id == 0
        last_row = row_id == RB - 1
        first_lane = lane_id == 0
        last_lane = lane_id == 127

        def pieces(ref, z, r):
            return tuple(ref[z, pl.ds(r, RB), pl.ds(128 * k, 128)] for k in range(npc))

        def step(src, dst, first):
            def level(z, accumulate):
                zu = jnp.minimum(z + 1, nz - 1)
                zl = jnp.maximum(z - 1, 0)
                k0 = jnp.where(z == 0, k0_first, k0_rest)
                ku = jnp.where(z == nz - 1, 0.0, diffusion + settling).astype(jnp.float32)

                def rot(b, c):
                    r = pl.multiple_of(b * RB, RB)
                    cur = pieces(src, z, r)
                    right = tuple(pltpu.roll(v, 1, 1) for v in cur)
                    left = tuple(pltpu.roll(v, 127, 1) for v in cur)
                    for k in range(npc):
                        s_buf[pl.ds(r, RB), pl.ds(128 * k, 128)] = jnp.where(
                            first_lane, right[(k - 1) % npc], right[k])
                        n_buf[pl.ds(r, RB), pl.ds(128 * k, 128)] = jnp.where(
                            last_lane, left[(k + 1) % npc], left[k])
                    return c

                lax.fori_loop(b_first, b_last + 1, rot, 0, unroll=True)

                def blk(b, carry, acc):
                    prev, cur = carry
                    r = pl.multiple_of(b * RB, RB)
                    nxt = pieces(src, z, r + RB)
                    up = pieces(src, zu, r)
                    low = pieces(src, zl, r)
                    o = pieces(o_buf, z, r)
                    ro = pl.multiple_of(r - PAD, RB)
                    for k in range(npc):
                        c = cur[k]
                        west = jnp.where(first_row, pltpu.roll(prev[k], 1, 0), pltpu.roll(c, 1, 0))
                        east = jnp.where(last_row, pltpu.roll(nxt[k], RB - 1, 0), pltpu.roll(c, RB - 1, 0))
                        south = s_buf[pl.ds(r, RB), pl.ds(128 * k, 128)]
                        north = n_buf[pl.ds(r, RB), pl.ds(128 * k, 128)]
                        new = o[k] * (
                            (k0 * c + k_w * west)
                            + (k_e * east + k_s * south)
                            + ((k_n * north + ku * up[k]) + diffusion * low[k])
                        )
                        dst[z, pl.ds(r, RB), pl.ds(128 * k, 128)] = new
                        if acc and k < nacc:
                            sq = new * new
                            if first:
                                out_ref[z, pl.ds(ro, RB), pl.ds(128 * k, 128)] = sq
                            else:
                                out_ref[z, pl.ds(ro, RB), pl.ds(128 * k, 128)] = (
                                    out_ref[z, pl.ds(ro, RB), pl.ds(128 * k, 128)] + sq
                                )
                    return (cur, nxt)

                carry = (pieces(src, z, 0), pieces(src, z, RB))
                if accumulate:
                    carry = lax.fori_loop(b_first, acc_lo, lambda b, c: blk(b, c, False), carry)
                    carry = lax.fori_loop(acc_lo, acc_hi, lambda b, c: blk(b, c, True), carry, unroll=True)
                    carry = lax.fori_loop(acc_hi, b_last + 1, lambda b, c: blk(b, c, False), carry)
                else:
                    carry = lax.fori_loop(b_first, b_last + 1, lambda b, c: blk(b, c, False), carry, unroll=True)

            def lvl_acc(z, c):
                level(z, True)
                return c

            def lvl_plain(z, c):
                level(z, False)
                return c

            lax.fori_loop(0, rz, lvl_acc, 0)
            lax.fori_loop(rz, nz, lvl_plain, 0)

        bufs = (a_buf, b_buf)
        for n in range(STEPS):
            step(bufs[n % 2], bufs[(n + 1) % 2], n == 0)

        def leth(z, c):
            for q in range(nh // 32):
                load = out_ref[z, pl.ds(q * 32, 32), :]
                probit = probit_a + probit_b * jnp.log(load + load_eps)
                lethal = 0.5 * (1.0 + lax.erf((probit - 5.0) / math.sqrt(2.0)))
                out_ref[z, pl.ds(q * 32, 32), :] = weight * lethal
            return c

        lax.fori_loop(0, rz, leth, 0)

    return kernel


def _reduce_sync(weighted):
    count = lax.axis_size("scen")
    parts = weighted.reshape((count, RZ // count) + weighted.shape[1:])
    return lax.all_to_all(parts, "scen", 0, 0, tiled=True).sum(0)


def on_device(source, obstacle, sector, freq_class):
    src = source[0]
    nz, nx, ny = src.shape
    courant_x, courant_y = wind_components(sector[0])
    weight = jnp.exp(-freq_rate * freq_class[0].astype(jnp.float32))
    px = jnp.maximum(courant_x, 0.0)
    mx = jnp.minimum(courant_x, 0.0)
    py = jnp.maximum(courant_y, 0.0)
    my = jnp.minimum(courant_y, 0.0)
    base = 1.0 - px + mx - py + my - 6.0 * diffusion
    coef = jnp.stack(
        [px + diffusion, diffusion - mx, py + diffusion, diffusion - my, base, base - settling,
         weight, jnp.float32(0.0)]
    ).astype(jnp.float32)
    r_lo, r_hi, lanes = ghost_pieces(src, obstacle)
    nh = nx // 2
    rows = nh + 2 * PAD
    width = ny + EXTRA
    any_spec = pl.BlockSpec(memory_space=pl.ANY)
    halves = []
    for half, ghost in ((0, r_lo), (1, r_hi)):
        halves.append(pl.pallas_call(
            make_kernel(nz, nx, ny, RZ, half),
            out_shape=jax.ShapeDtypeStruct((RZ, nh, ny), jnp.float32),
            in_specs=[pl.BlockSpec(memory_space=pltpu.SMEM)] + [any_spec] * 4,
            out_specs=pl.BlockSpec(memory_space=pltpu.VMEM),
            scratch_shapes=[
                pltpu.VMEM((nz, rows, width), jnp.float32),
                pltpu.VMEM((nz, rows, width), jnp.float32),
                pltpu.VMEM((nz, rows, width), jnp.float32),
                pltpu.VMEM((nz, nh + PAD, ny), jnp.int32),
                pltpu.SemaphoreType.DMA((8,)),
                pltpu.VMEM((rows, width), jnp.float32),
                pltpu.VMEM((rows, width), jnp.float32),
            ],
            compiler_params=pltpu.CompilerParams(vmem_limit_bytes=62 * 1024 * 1024),
        )(coef, source, obstacle, ghost, lanes))
        if half == 0:
            first = _reduce_sync(halves[0])
    second = _reduce_sync(halves[1])
    return jnp.concatenate([first, second], axis=1)


def solution(mesh):
    in_specs = (P("scen", None, "gx", "gy"), P(None, "gx", "gy"), P("scen"), P("scen"))
    out_specs = P("scen", "gx", "gy")
    return jax.shard_map(
        on_device, mesh=mesh, in_specs=in_specs, out_specs=out_specs, check_vma=False
    )
```

```python
import math

import jax
import jax.numpy as jnp
from jax import lax
from jax.experimental import pallas as pl
from jax.experimental.pallas import tpu as pltpu
from jax.sharding import PartitionSpec as P

STEPS = 4
RZ = 16


wind_speed = 0.4
diffusion = 0.05
settling = 0.1
probit_a = 3.0
probit_b = 1.0
load_eps = 0.01
freq_rate = 0.7

H = STEPS
PAD = 16
EXTRA = 128
RB = 8


def wind_components(sector_id):
    heading = sector_id.astype(jnp.float32) * (2.0 * math.pi / 16.0)
    return (wind_speed * jnp.cos(heading), wind_speed * jnp.sin(heading))


def _open_and_c(src, obs):
    open_cells = (1 - obs).astype(jnp.float32)
    return jnp.stack([src * open_cells, open_cells])


def _select(count, width, picks):
    cols = jnp.asarray(picks, jnp.int32)[:, None]
    return (lax.broadcasted_iota(jnp.int32, (count, width), 1) == cols).astype(jnp.float32)


def _split3(x):
    def bf(v):
        return lax.reduce_precision(v, exponent_bits=8, mantissa_bits=7)

    top = bf(x)
    rest = x - top
    mid = bf(rest)
    low = rest - mid
    return (top.astype(jnp.bfloat16), mid.astype(jnp.bfloat16), low.astype(jnp.bfloat16))


def ghost_pieces(src, obs):
    nz, nx, ny = src.shape
    gxn = lax.axis_size("gx")
    gyn = lax.axis_size("gy")
    fx = [(i, i + 1) for i in range(gxn - 1)]
    bx = [(i + 1, i) for i in range(gxn - 1)]
    fy = [(i, i + 1) for i in range(gyn - 1)]
    by = [(i + 1, i) for i in range(gyn - 1)]
    hi = lax.Precision.HIGHEST
    last_rows = _open_and_c(src[:, nx - H:, :], obs[:, nx - H:, :])
    first_rows = _open_and_c(src[:, :H, :], obs[:, :H, :])
    xlo = lax.ppermute(last_rows, "gx", fx)
    xhi = lax.ppermute(first_rows, "gx", bx)
    pick = _select(2 * H, ny, list(range(H)) + list(range(ny - H, ny)))
    src_cols = jnp.einsum("zxy,ky->zkx", src, pick, precision=hi)
    open_cols = jnp.einsum(
        "zxy,ky->zkx", (1 - obs).astype(jnp.bfloat16), pick.astype(jnp.bfloat16),
        preferred_element_type=jnp.float32)
    cols = jnp.stack([src_cols * open_cols, open_cols])
    corner_lo = jnp.swapaxes(jnp.concatenate([xlo[..., :H], xlo[..., ny - H:]], -1), -1, -2)
    corner_hi = jnp.swapaxes(jnp.concatenate([xhi[..., :H], xhi[..., ny - H:]], -1), -1, -2)
    ext = jnp.concatenate([corner_lo, cols, corner_hi], axis=-1)
    yw = lax.ppermute(ext[:, :, H:], "gy", fy)
    ye = lax.ppermute(ext[:, :, :H], "gy", by)
    rows = nx + 2 * PAD
    yt = jnp.concatenate([ye, yw], axis=2)
    yt = jnp.pad(yt, ((0, 0), (0, 0), (0, 0), (PAD - H, rows - nx - PAD - H)))
    place = _select(2 * H, EXTRA, list(range(H)) + list(range(EXTRA - H, EXTRA)))
    place = jnp.concatenate([place] * 3, 0).astype(jnp.bfloat16)
    lanes = jnp.einsum(
        "czkr,kj->czrj", jnp.concatenate(_split3(yt), 2), place,
        preferred_element_type=jnp.float32)
    r_lo = jnp.pad(xlo, ((0, 0), (0, 0), (PAD - H, 0), (0, 0)))
    r_hi = jnp.pad(xhi, ((0, 0), (0, 0), (0, PAD - H), (0, 0)))
    return r_lo, r_hi, lanes


def make_kernel(nz, nx, ny, rz, xs, nh):
    half = 0 if xs == 0 else 1
    rows = nh + 2 * PAD
    width = ny + EXTRA
    nblk = rows // RB
    b_first = 1
    b_last = nblk - 2
    acc_lo = PAD // RB
    acc_hi = (PAD + nh) // RB
    s0 = max(0, xs - PAD)
    nb = min(nx, xs + nh + PAD) - s0
    b0 = s0 - (xs - PAD)
    g0 = 0 if half == 0 else PAD + nh
    lane0 = xs

    def kernel(coef, src_hbm, obs_hbm, ghost_hbm, lanes_hbm, out_ref,
               a_buf, b_buf, o_buf, obs_buf, sems, s_buf, n_buf):
        copies = [
            pltpu.make_async_copy(obs_hbm.at[:, pl.ds(s0, nb), :], obs_buf, sems.at[0]),
            pltpu.make_async_copy(ghost_hbm.at[1], o_buf.at[:, pl.ds(g0, PAD), pl.ds(0, ny)], sems.at[1]),
            pltpu.make_async_copy(lanes_hbm.at[1, :, pl.ds(lane0, rows)], o_buf.at[:, :, pl.ds(ny, EXTRA)], sems.at[3]),
            pltpu.make_async_copy(src_hbm.at[0, :, pl.ds(s0, nb), :], a_buf.at[:, pl.ds(b0, nb), pl.ds(0, ny)], sems.at[4]),
            pltpu.make_async_copy(ghost_hbm.at[0], a_buf.at[:, pl.ds(g0, PAD), pl.ds(0, ny)], sems.at[5]),
            pltpu.make_async_copy(lanes_hbm.at[0, :, pl.ds(lane0, rows)], a_buf.at[:, :, pl.ds(ny, EXTRA)], sems.at[7]),
        ]
        for cp in copies:
            cp.start()

        zeros = jnp.zeros((RB, width), jnp.float32)

        def clear(z, c):
            b_buf[z, pl.ds(0, RB), :] = zeros
            b_buf[z, pl.ds(rows - RB, RB), :] = zeros
            return c

        lax.fori_loop(0, nz, clear, 0)

        copies[0].wait()

        def to_open(z, c):
            o_buf[z, pl.ds(b0, nb), pl.ds(0, ny)] = (1 - obs_buf[z]).astype(jnp.float32)
            return c

        lax.fori_loop(0, nz, to_open, 0)
        copies[3].wait()

        def to_c0(z, c):
            a_buf[z, pl.ds(b0, nb), pl.ds(0, ny)] = (
                a_buf[z, pl.ds(b0, nb), pl.ds(0, ny)] * o_buf[z, pl.ds(b0, nb), pl.ds(0, ny)]
            )
            return c

        lax.fori_loop(0, nz, to_c0, 0)
        for cp in copies[1:3] + copies[4:]:
            cp.wait()

        k_w = coef[0]
        k_e = coef[1]
        k_s = coef[2]
        k_n = coef[3]
        k0_first = coef[4]
        k0_rest = coef[5]
        weight = coef[6]
        npc = width // 128
        nacc = ny // 128
        row_id = lax.broadcasted_iota(jnp.int32, (RB, 128), 0)
        lane_id = lax.broadcasted_iota(jnp.int32, (RB, 128), 1)
        first_row = row_id == 0
        last_row = row_id == RB - 1
        first_lane = lane_id == 0
        last_lane = lane_id == 127

        def pieces(ref, z, r):
            return tuple(ref[z, pl.ds(r, RB), pl.ds(128 * k, 128)] for k in range(npc))

        def step(src, dst, first):
            def level(z, accumulate):
                zu = jnp.minimum(z + 1, nz - 1)
                zl = jnp.maximum(z - 1, 0)
                k0 = jnp.where(z == 0, k0_first, k0_rest)
                ku = jnp.where(z == nz - 1, 0.0, diffusion + settling).astype(jnp.float32)

                def rot(b, c):
                    r = pl.multiple_of(b * RB, RB)
                    cur = pieces(src, z, r)
                    right = tuple(pltpu.roll(v, 1, 1) for v in cur)
                    left = tuple(pltpu.roll(v, 127, 1) for v in cur)
                    for k in range(npc):
                        s_buf[pl.ds(r, RB), pl.ds(128 * k, 128)] = jnp.where(
                            first_lane, right[(k - 1) % npc], right[k])
                        n_buf[pl.ds(r, RB), pl.ds(128 * k, 128)] = jnp.where(
                            last_lane, left[(k + 1) % npc], left[k])
                    return c

                lax.fori_loop(b_first, b_last + 1, rot, 0, unroll=True)

                def blk(b, carry, acc):
                    prev, cur = carry
                    r = pl.multiple_of(b * RB, RB)
                    nxt = pieces(src, z, r + RB)
                    up = pieces(src, zu, r)
                    low = pieces(src, zl, r)
                    o = pieces(o_buf, z, r)
                    ro = pl.multiple_of(r - PAD, RB)
                    for k in range(npc):
                        c = cur[k]
                        west = jnp.where(first_row, pltpu.roll(prev[k], 1, 0), pltpu.roll(c, 1, 0))
                        east = jnp.where(last_row, pltpu.roll(nxt[k], RB - 1, 0), pltpu.roll(c, RB - 1, 0))
                        south = s_buf[pl.ds(r, RB), pl.ds(128 * k, 128)]
                        north = n_buf[pl.ds(r, RB), pl.ds(128 * k, 128)]
                        new = o[k] * (
                            (k0 * c + k_w * west)
                            + (k_e * east + k_s * south)
                            + ((k_n * north + ku * up[k]) + diffusion * low[k])
                        )
                        dst[z, pl.ds(r, RB), pl.ds(128 * k, 128)] = new
                        if acc and k < nacc:
                            sq = new * new
                            if first:
                                out_ref[z, pl.ds(ro, RB), pl.ds(128 * k, 128)] = sq
                            else:
                                out_ref[z, pl.ds(ro, RB), pl.ds(128 * k, 128)] = (
                                    out_ref[z, pl.ds(ro, RB), pl.ds(128 * k, 128)] + sq
                                )
                    return (cur, nxt)

                carry = (pieces(src, z, 0), pieces(src, z, RB))
                if accumulate:
                    carry = lax.fori_loop(b_first, acc_lo, lambda b, c: blk(b, c, False), carry)
                    carry = lax.fori_loop(acc_lo, acc_hi, lambda b, c: blk(b, c, True), carry, unroll=True)
                    carry = lax.fori_loop(acc_hi, b_last + 1, lambda b, c: blk(b, c, False), carry)
                else:
                    carry = lax.fori_loop(b_first, b_last + 1, lambda b, c: blk(b, c, False), carry, unroll=True)

            def lvl_acc(z, c):
                level(z, True)
                return c

            def lvl_plain(z, c):
                level(z, False)
                return c

            lax.fori_loop(0, rz, lvl_acc, 0)
            lax.fori_loop(rz, nz, lvl_plain, 0)

        bufs = (a_buf, b_buf)
        for n in range(STEPS):
            step(bufs[n % 2], bufs[(n + 1) % 2], n == 0)

        def leth(z, c):
            for q in range(nh // 16):
                load = out_ref[z, pl.ds(q * 16, 16), :]
                probit = probit_a + probit_b * jnp.log(load + load_eps)
                lethal = 0.5 * (1.0 + lax.erf((probit - 5.0) / math.sqrt(2.0)))
                out_ref[z, pl.ds(q * 16, 16), :] = weight * lethal
            return c

        lax.fori_loop(0, rz, leth, 0)

    return kernel


def _reduce_sync(weighted):
    count = lax.axis_size("scen")
    parts = weighted.reshape((count, RZ // count) + weighted.shape[1:])
    return lax.all_to_all(parts, "scen", 0, 0, tiled=True).sum(0)


def on_device(source, obstacle, sector, freq_class):
    src = source[0]
    nz, nx, ny = src.shape
    courant_x, courant_y = wind_components(sector[0])
    weight = jnp.exp(-freq_rate * freq_class[0].astype(jnp.float32))
    px = jnp.maximum(courant_x, 0.0)
    mx = jnp.minimum(courant_x, 0.0)
    py = jnp.maximum(courant_y, 0.0)
    my = jnp.minimum(courant_y, 0.0)
    base = 1.0 - px + mx - py + my - 6.0 * diffusion
    coef = jnp.stack(
        [px + diffusion, diffusion - mx, py + diffusion, diffusion - my, base, base - settling,
         weight, jnp.float32(0.0)]
    ).astype(jnp.float32)
    r_lo, r_hi, lanes = ghost_pieces(src, obstacle)
    first_rows = (nx // 2 + 16) // 16 * 16
    width = ny + EXTRA
    any_spec = pl.BlockSpec(memory_space=pl.ANY)
    halves = []
    for half, ghost, xs, nh in ((0, r_lo, 0, first_rows), (1, r_hi, first_rows, nx - first_rows)):
        rows = nh + 2 * PAD
        nb = min(nx, xs + nh + PAD) - max(0, xs - PAD)
        halves.append(pl.pallas_call(
            make_kernel(nz, nx, ny, RZ, xs, nh),
            out_shape=jax.ShapeDtypeStruct((RZ, nh, ny), jnp.float32),
            in_specs=[pl.BlockSpec(memory_space=pltpu.SMEM)] + [any_spec] * 4,
            out_specs=pl.BlockSpec(memory_space=pltpu.VMEM),
            scratch_shapes=[
                pltpu.VMEM((nz, rows, width), jnp.float32),
                pltpu.VMEM((nz, rows, width), jnp.float32),
                pltpu.VMEM((nz, rows, width), jnp.float32),
                pltpu.VMEM((nz, nb, ny), jnp.int32),
                pltpu.SemaphoreType.DMA((8,)),
                pltpu.VMEM((rows, width), jnp.float32),
                pltpu.VMEM((rows, width), jnp.float32),
            ],
            compiler_params=pltpu.CompilerParams(vmem_limit_bytes=62 * 1024 * 1024),
        )(coef, source, obstacle, ghost, lanes))
        if half == 0:
            first = _reduce_sync(halves[0])
    second = _reduce_sync(halves[1])
    return jnp.concatenate([first, second], axis=1)


def solution(mesh):
    in_specs = (P("scen", None, "gx", "gy"), P(None, "gx", "gy"), P("scen"), P("scen"))
    out_specs = P("scen", "gx", "gy")
    return jax.shard_map(
        on_device, mesh=mesh, in_specs=in_specs, out_specs=out_specs, check_vma=False
    )
```

```python
import math

import jax
import jax.numpy as jnp
from jax import lax
from jax.experimental import pallas as pl
from jax.experimental.pallas import tpu as pltpu
from jax.sharding import PartitionSpec as P

STEPS = 4
RZ = 16


wind_speed = 0.4
diffusion = 0.05
settling = 0.1
probit_a = 3.0
probit_b = 1.0
load_eps = 0.01
freq_rate = 0.7

H = STEPS
PAD = 16
EXTRA = 128
RB = 8


def wind_components(sector_id):
    heading = sector_id.astype(jnp.float32) * (2.0 * math.pi / 16.0)
    return (wind_speed * jnp.cos(heading), wind_speed * jnp.sin(heading))


def _open_and_c(src, obs):
    open_cells = (1 - obs).astype(jnp.float32)
    return jnp.stack([src * open_cells, open_cells])


def _select(count, width, picks):
    cols = jnp.asarray(picks, jnp.int32)[:, None]
    return (lax.broadcasted_iota(jnp.int32, (count, width), 1) == cols).astype(jnp.float32)


def _split3(x):
    def bf(v):
        return lax.reduce_precision(v, exponent_bits=8, mantissa_bits=7)

    top = bf(x)
    rest = x - top
    mid = bf(rest)
    low = rest - mid
    return (top.astype(jnp.bfloat16), mid.astype(jnp.bfloat16), low.astype(jnp.bfloat16))


def ghost_pieces(src, obs):
    nz, nx, ny = src.shape
    gxn = lax.axis_size("gx")
    gyn = lax.axis_size("gy")
    fx = [(i, i + 1) for i in range(gxn - 1)]
    bx = [(i + 1, i) for i in range(gxn - 1)]
    fy = [(i, i + 1) for i in range(gyn - 1)]
    by = [(i + 1, i) for i in range(gyn - 1)]
    hi = lax.Precision.HIGHEST
    last_rows = _open_and_c(src[:, nx - H:, :], obs[:, nx - H:, :])
    first_rows = _open_and_c(src[:, :H, :], obs[:, :H, :])
    xlo = lax.ppermute(last_rows, "gx", fx)
    xhi = lax.ppermute(first_rows, "gx", bx)
    pick = _select(2 * H, ny, list(range(H)) + list(range(ny - H, ny)))
    src_cols = jnp.einsum("zxy,ky->zkx", src, pick, precision=hi)
    open_cols = jnp.einsum(
        "zxy,ky->zkx", (1 - obs).astype(jnp.bfloat16), pick.astype(jnp.bfloat16),
        preferred_element_type=jnp.float32)
    cols = jnp.stack([src_cols * open_cols, open_cols])
    corner_lo = jnp.swapaxes(jnp.concatenate([xlo[..., :H], xlo[..., ny - H:]], -1), -1, -2)
    corner_hi = jnp.swapaxes(jnp.concatenate([xhi[..., :H], xhi[..., ny - H:]], -1), -1, -2)
    ext = jnp.concatenate([corner_lo, cols, corner_hi], axis=-1)
    yw = lax.ppermute(ext[:, :, H:], "gy", fy)
    ye = lax.ppermute(ext[:, :, :H], "gy", by)
    rows = nx + 2 * PAD
    yt = jnp.concatenate([ye, yw], axis=2)
    yt = jnp.pad(yt, ((0, 0), (0, 0), (0, 0), (PAD - H, rows - nx - PAD - H)))
    place = _select(2 * H, EXTRA, list(range(H)) + list(range(EXTRA - H, EXTRA)))
    place = jnp.concatenate([place] * 3, 0).astype(jnp.bfloat16)
    lanes = jnp.einsum(
        "czkr,kj->czrj", jnp.concatenate(_split3(yt), 2), place,
        preferred_element_type=jnp.float32)
    return xlo, xhi, lanes


def make_kernel(nz, nx, ny, rz, half):
    nh = nx // 2
    rows = nh + 2 * PAD
    width = ny + EXTRA
    nblk = rows // RB
    b_first = 1
    b_last = nblk - 2
    acc_lo = PAD // RB
    acc_hi = (PAD + nh) // RB
    nb = nh + PAD
    s0 = 0 if half == 0 else nx - nb
    b0 = PAD if half == 0 else 0
    g0 = PAD - H if half == 0 else nb
    lane0 = 0 if half == 0 else nh

    def kernel(coef, src_hbm, obs_hbm, ghost_hbm, lanes_hbm, out_ref,
               a_buf, b_buf, o_buf, obs_buf, sems, s_buf, n_buf):
        copies = [
            pltpu.make_async_copy(obs_hbm.at[:, pl.ds(s0, nb), :], obs_buf, sems.at[0]),
            pltpu.make_async_copy(ghost_hbm.at[1], o_buf.at[:, pl.ds(g0, H), pl.ds(0, ny)], sems.at[1]),
            pltpu.make_async_copy(lanes_hbm.at[1, :, pl.ds(lane0, rows)], o_buf.at[:, :, pl.ds(ny, EXTRA)], sems.at[3]),
            pltpu.make_async_copy(src_hbm.at[0, :, pl.ds(s0, nb), :], a_buf.at[:, pl.ds(b0, nb), pl.ds(0, ny)], sems.at[4]),
            pltpu.make_async_copy(ghost_hbm.at[0], a_buf.at[:, pl.ds(g0, H), pl.ds(0, ny)], sems.at[5]),
            pltpu.make_async_copy(lanes_hbm.at[0, :, pl.ds(lane0, rows)], a_buf.at[:, :, pl.ds(ny, EXTRA)], sems.at[7]),
        ]
        for cp in copies:
            cp.start()

        zeros = jnp.zeros((RB, width), jnp.float32)

        def clear(z, c):
            b_buf[z, pl.ds(0, RB), :] = zeros
            b_buf[z, pl.ds(rows - RB, RB), :] = zeros
            return c

        lax.fori_loop(0, nz, clear, 0)

        copies[0].wait()

        def to_open(z, c):
            o_buf[z, pl.ds(b0, nb), pl.ds(0, ny)] = (1 - obs_buf[z]).astype(jnp.float32)
            return c

        lax.fori_loop(0, nz, to_open, 0)
        copies[3].wait()

        def to_c0(z, c):
            a_buf[z, pl.ds(b0, nb), pl.ds(0, ny)] = (
                a_buf[z, pl.ds(b0, nb), pl.ds(0, ny)] * o_buf[z, pl.ds(b0, nb), pl.ds(0, ny)]
            )
            return c

        lax.fori_loop(0, nz, to_c0, 0)
        for cp in copies[1:3] + copies[4:]:
            cp.wait()

        k_w = coef[0]
        k_e = coef[1]
        k_s = coef[2]
        k_n = coef[3]
        k0_first = coef[4]
        k0_rest = coef[5]
        weight = coef[6]
        npc = width // 128
        nacc = ny // 128
        row_id = lax.broadcasted_iota(jnp.int32, (RB, 128), 0)
        lane_id = lax.broadcasted_iota(jnp.int32, (RB, 128), 1)
        first_row = row_id == 0
        last_row = row_id == RB - 1
        first_lane = lane_id == 0
        last_lane = lane_id == 127

        def pieces(ref, z, r):
            return tuple(ref[z, pl.ds(r, RB), pl.ds(128 * k, 128)] for k in range(npc))

        def step(src, dst, first):
            def level(z, accumulate):
                zu = jnp.minimum(z + 1, nz - 1)
                zl = jnp.maximum(z - 1, 0)
                k0 = jnp.where(z == 0, k0_first, k0_rest)
                ku = jnp.where(z == nz - 1, 0.0, diffusion + settling).astype(jnp.float32)

                def rot(b, c):
                    r = pl.multiple_of(b * RB, RB)
                    cur = pieces(src, z, r)
                    right = tuple(pltpu.roll(v, 1, 1) for v in cur)
                    left = tuple(pltpu.roll(v, 127, 1) for v in cur)
                    for k in range(npc):
                        s_buf[pl.ds(r, RB), pl.ds(128 * k, 128)] = jnp.where(
                            first_lane, right[(k - 1) % npc], right[k])
                        n_buf[pl.ds(r, RB), pl.ds(128 * k, 128)] = jnp.where(
                            last_lane, left[(k + 1) % npc], left[k])
                    return c

                lax.fori_loop(b_first, b_last + 1, rot, 0, unroll=True)

                def blk(b, carry, acc):
                    prev, cur = carry
                    r = pl.multiple_of(b * RB, RB)
                    nxt = pieces(src, z, r + RB)
                    up = pieces(src, zu, r)
                    low = pieces(src, zl, r)
                    o = pieces(o_buf, z, r)
                    ro = pl.multiple_of(r - PAD, RB)
                    for k in range(npc):
                        c = cur[k]
                        west = jnp.where(first_row, pltpu.roll(prev[k], 1, 0), pltpu.roll(c, 1, 0))
                        east = jnp.where(last_row, pltpu.roll(nxt[k], RB - 1, 0), pltpu.roll(c, RB - 1, 0))
                        south = s_buf[pl.ds(r, RB), pl.ds(128 * k, 128)]
                        north = n_buf[pl.ds(r, RB), pl.ds(128 * k, 128)]
                        new = o[k] * (
                            (k0 * c + k_w * west)
                            + (k_e * east + k_s * south)
                            + ((k_n * north + ku * up[k]) + diffusion * low[k])
                        )
                        dst[z, pl.ds(r, RB), pl.ds(128 * k, 128)] = new
                        if acc and k < nacc:
                            sq = new * new
                            if first:
                                out_ref[z, pl.ds(ro, RB), pl.ds(128 * k, 128)] = sq
                            else:
                                out_ref[z, pl.ds(ro, RB), pl.ds(128 * k, 128)] = (
                                    out_ref[z, pl.ds(ro, RB), pl.ds(128 * k, 128)] + sq
                                )
                    return (cur, nxt)

                carry = (pieces(src, z, 0), pieces(src, z, RB))
                if accumulate:
                    carry = lax.fori_loop(b_first, acc_lo, lambda b, c: blk(b, c, False), carry)
                    carry = lax.fori_loop(acc_lo, acc_hi, lambda b, c: blk(b, c, True), carry, unroll=True)
                    carry = lax.fori_loop(acc_hi, b_last + 1, lambda b, c: blk(b, c, False), carry)
                else:
                    carry = lax.fori_loop(b_first, b_last + 1, lambda b, c: blk(b, c, False), carry, unroll=True)

            def lvl_acc(z, c):
                level(z, True)
                return c

            def lvl_plain(z, c):
                level(z, False)
                return c

            lax.fori_loop(0, rz, lvl_acc, 0)
            lax.fori_loop(rz, nz, lvl_plain, 0)

        bufs = (a_buf, b_buf)
        for n in range(STEPS):
            step(bufs[n % 2], bufs[(n + 1) % 2], n == 0)

        def leth(z, c):
            for q in range(nh // 32):
                load = out_ref[z, pl.ds(q * 32, 32), :]
                probit = probit_a + probit_b * jnp.log(load + load_eps)
                lethal = 0.5 * (1.0 + lax.erf((probit - 5.0) / math.sqrt(2.0)))
                out_ref[z, pl.ds(q * 32, 32), :] = weight * lethal
            return c

        lax.fori_loop(0, rz, leth, 0)

    return kernel


def _reduce_sync(weighted):
    count = lax.axis_size("scen")
    parts = weighted.reshape((count, RZ // count) + weighted.shape[1:])
    return lax.all_to_all(parts, "scen", 0, 0, tiled=True).sum(0)


def on_device(source, obstacle, sector, freq_class):
    src = source[0]
    nz, nx, ny = src.shape
    courant_x, courant_y = wind_components(sector[0])
    weight = jnp.exp(-freq_rate * freq_class[0].astype(jnp.float32))
    px = jnp.maximum(courant_x, 0.0)
    mx = jnp.minimum(courant_x, 0.0)
    py = jnp.maximum(courant_y, 0.0)
    my = jnp.minimum(courant_y, 0.0)
    base = 1.0 - px + mx - py + my - 6.0 * diffusion
    coef = jnp.stack(
        [px + diffusion, diffusion - mx, py + diffusion, diffusion - my, base, base - settling,
         weight, jnp.float32(0.0)]
    ).astype(jnp.float32)
    r_lo, r_hi, lanes = ghost_pieces(src, obstacle)
    nh = nx // 2
    rows = nh + 2 * PAD
    width = ny + EXTRA
    any_spec = pl.BlockSpec(memory_space=pl.ANY)
    halves = []
    for half, ghost in ((0, r_lo), (1, r_hi)):
        halves.append(pl.pallas_call(
            make_kernel(nz, nx, ny, RZ, half),
            out_shape=jax.ShapeDtypeStruct((RZ, nh, ny), jnp.float32),
            in_specs=[pl.BlockSpec(memory_space=pltpu.SMEM)] + [any_spec] * 4,
            out_specs=pl.BlockSpec(memory_space=pltpu.VMEM),
            scratch_shapes=[
                pltpu.VMEM((nz, rows, width), jnp.float32),
                pltpu.VMEM((nz, rows, width), jnp.float32),
                pltpu.VMEM((nz, rows, width), jnp.float32),
                pltpu.VMEM((nz, nh + PAD, ny), jnp.int32),
                pltpu.SemaphoreType.DMA((8,)),
                pltpu.VMEM((rows, width), jnp.float32),
                pltpu.VMEM((rows, width), jnp.float32),
            ],
            compiler_params=pltpu.CompilerParams(vmem_limit_bytes=62 * 1024 * 1024),
        )(coef, source, obstacle, ghost, lanes))
        if half == 0:
            first = _reduce_sync(halves[0])
    second = _reduce_sync(halves[1])
    return jnp.concatenate([first, second], axis=1)


def solution(mesh):
    in_specs = (P("scen", None, "gx", "gy"), P(None, "gx", "gy"), P("scen"), P("scen"))
    out_specs = P("scen", "gx", "gy")
    return jax.shard_map(
        on_device, mesh=mesh, in_specs=in_specs, out_specs=out_specs, check_vma=False
    )
```

```python
import math

import jax
import jax.numpy as jnp
from jax import lax
from jax.experimental import pallas as pl
from jax.experimental.pallas import tpu as pltpu
from jax.sharding import PartitionSpec as P

STEPS = 4
RZ = 16


wind_speed = 0.4
diffusion = 0.05
settling = 0.1
probit_a = 3.0
probit_b = 1.0
load_eps = 0.01
freq_rate = 0.7

H = STEPS
PAD = 16
EXTRA = 128
RB = 8


def wind_components(sector_id):
    heading = sector_id.astype(jnp.float32) * (2.0 * math.pi / 16.0)
    return (wind_speed * jnp.cos(heading), wind_speed * jnp.sin(heading))


def _open_and_c(src, obs):
    open_cells = (1 - obs).astype(jnp.float32)
    return jnp.stack([src * open_cells, open_cells])


def _select(count, width, picks):
    cols = jnp.asarray(picks, jnp.int32)[:, None]
    return (lax.broadcasted_iota(jnp.int32, (count, width), 1) == cols).astype(jnp.float32)


def _split3(x):
    def bf(v):
        return lax.reduce_precision(v, exponent_bits=8, mantissa_bits=7)

    top = bf(x)
    rest = x - top
    mid = bf(rest)
    low = rest - mid
    return (top.astype(jnp.bfloat16), mid.astype(jnp.bfloat16), low.astype(jnp.bfloat16))


def ghost_pieces(src, obs):
    nz, nx, ny = src.shape
    gxn = lax.axis_size("gx")
    gyn = lax.axis_size("gy")
    fx = [(i, i + 1) for i in range(gxn - 1)]
    bx = [(i + 1, i) for i in range(gxn - 1)]
    fy = [(i, i + 1) for i in range(gyn - 1)]
    by = [(i + 1, i) for i in range(gyn - 1)]
    hi = lax.Precision.HIGHEST
    last_rows = _open_and_c(src[:, nx - H:, :], obs[:, nx - H:, :])
    first_rows = _open_and_c(src[:, :H, :], obs[:, :H, :])
    xlo = lax.ppermute(last_rows, "gx", fx)
    xhi = lax.ppermute(first_rows, "gx", bx)
    pick = _select(2 * H, ny, list(range(H)) + list(range(ny - H, ny)))
    src_cols = jnp.einsum("zxy,ky->zkx", src, pick, precision=hi)
    open_cols = jnp.einsum(
        "zxy,ky->zkx", (1 - obs).astype(jnp.bfloat16), pick.astype(jnp.bfloat16),
        preferred_element_type=jnp.float32)
    cols = jnp.stack([src_cols * open_cols, open_cols])
    corner_lo = jnp.swapaxes(jnp.concatenate([xlo[..., :H], xlo[..., ny - H:]], -1), -1, -2)
    corner_hi = jnp.swapaxes(jnp.concatenate([xhi[..., :H], xhi[..., ny - H:]], -1), -1, -2)
    ext = jnp.concatenate([corner_lo, cols, corner_hi], axis=-1)
    yw = lax.ppermute(ext[:, :, H:], "gy", fy)
    ye = lax.ppermute(ext[:, :, :H], "gy", by)
    rows = nx + 2 * PAD
    yt = jnp.concatenate([ye, yw], axis=2)
    yt = jnp.pad(yt, ((0, 0), (0, 0), (0, 0), (PAD - H, rows - nx - PAD - H)))
    place = _select(2 * H, EXTRA, list(range(H)) + list(range(EXTRA - H, EXTRA)))
    place = jnp.concatenate([place] * 3, 0).astype(jnp.bfloat16)
    lanes = jnp.einsum(
        "czkr,kj->czrj", jnp.concatenate(_split3(yt), 2), place,
        preferred_element_type=jnp.float32)
    return xlo, xhi, lanes


def make_kernel(nz, nx, ny, rz, half):
    nh = nx // 2
    rows = nh + 2 * PAD
    width = ny + EXTRA
    nblk = rows // RB
    b_first = 1
    b_last = nblk - 2
    acc_lo = PAD // RB
    acc_hi = (PAD + nh) // RB
    nb = nh + PAD
    s0 = 0 if half == 0 else nx - nb
    b0 = PAD if half == 0 else 0
    g0 = PAD - H if half == 0 else nb
    lane0 = 0 if half == 0 else nh

    def kernel(coef, src_hbm, obs_hbm, ghost_hbm, lanes_hbm, out_ref,
               a_buf, b_buf, o_buf, obs_buf, sems, s_buf, n_buf):
        groups = 4
        per = nz // groups
        obs_cp = [
            pltpu.make_async_copy(
                obs_hbm.at[pl.ds(g * per, per), pl.ds(s0, nb), :],
                obs_buf.at[pl.ds(g * per, per)], sems.at[g])
            for g in range(groups)
        ]
        src_cp = [
            pltpu.make_async_copy(
                src_hbm.at[0, pl.ds(g * per, per), pl.ds(s0, nb), :],
                a_buf.at[pl.ds(g * per, per), pl.ds(b0, nb), pl.ds(0, ny)], sems.at[groups + g])
            for g in range(groups)
        ]
        rest = [
            pltpu.make_async_copy(ghost_hbm.at[1], o_buf.at[:, pl.ds(g0, H), pl.ds(0, ny)], sems.at[2 * groups]),
            pltpu.make_async_copy(ghost_hbm.at[0], a_buf.at[:, pl.ds(g0, H), pl.ds(0, ny)], sems.at[2 * groups + 1]),
            pltpu.make_async_copy(lanes_hbm.at[1, :, pl.ds(lane0, rows)], o_buf.at[:, :, pl.ds(ny, EXTRA)], sems.at[2 * groups + 2]),
            pltpu.make_async_copy(lanes_hbm.at[0, :, pl.ds(lane0, rows)], a_buf.at[:, :, pl.ds(ny, EXTRA)], sems.at[2 * groups + 3]),
        ]
        for g in range(groups):
            obs_cp[g].start()
            src_cp[g].start()
        for cp in rest:
            cp.start()

        zeros = jnp.zeros((RB, width), jnp.float32)

        def clear(z, c):
            b_buf[z, pl.ds(0, RB), :] = zeros
            b_buf[z, pl.ds(rows - RB, RB), :] = zeros
            return c

        lax.fori_loop(0, nz, clear, 0)

        def to_open(z, c):
            o_buf[z, pl.ds(b0, nb), pl.ds(0, ny)] = (1 - obs_buf[z]).astype(jnp.float32)
            return c

        def to_c0(z, c):
            a_buf[z, pl.ds(b0, nb), pl.ds(0, ny)] = (
                a_buf[z, pl.ds(b0, nb), pl.ds(0, ny)] * o_buf[z, pl.ds(b0, nb), pl.ds(0, ny)]
            )
            return c

        for g in range(groups):
            obs_cp[g].wait()
            lax.fori_loop(g * per, (g + 1) * per, to_open, 0)
            src_cp[g].wait()
            lax.fori_loop(g * per, (g + 1) * per, to_c0, 0)
        for cp in rest:
            cp.wait()

        k_w = coef[0]
        k_e = coef[1]
        k_s = coef[2]
        k_n = coef[3]
        k0_first = coef[4]
        k0_rest = coef[5]
        weight = coef[6]
        npc = width // 128
        nacc = ny // 128
        row_id = lax.broadcasted_iota(jnp.int32, (RB, 128), 0)
        lane_id = lax.broadcasted_iota(jnp.int32, (RB, 128), 1)
        first_row = row_id == 0
        last_row = row_id == RB - 1
        first_lane = lane_id == 0
        last_lane = lane_id == 127

        def pieces(ref, z, r):
            return tuple(ref[z, pl.ds(r, RB), pl.ds(128 * k, 128)] for k in range(npc))

        def step(src, dst, first):
            def level(z, accumulate):
                zu = jnp.minimum(z + 1, nz - 1)
                zl = jnp.maximum(z - 1, 0)
                k0 = jnp.where(z == 0, k0_first, k0_rest)
                ku = jnp.where(z == nz - 1, 0.0, diffusion + settling).astype(jnp.float32)

                def rot(b, c):
                    r = pl.multiple_of(b * RB, RB)
                    cur = pieces(src, z, r)
                    right = tuple(pltpu.roll(v, 1, 1) for v in cur)
                    left = tuple(pltpu.roll(v, 127, 1) for v in cur)
                    for k in range(npc):
                        s_buf[pl.ds(r, RB), pl.ds(128 * k, 128)] = jnp.where(
                            first_lane, right[(k - 1) % npc], right[k])
                        n_buf[pl.ds(r, RB), pl.ds(128 * k, 128)] = jnp.where(
                            last_lane, left[(k + 1) % npc], left[k])
                    return c

                lax.fori_loop(b_first, b_last + 1, rot, 0, unroll=True)

                def blk(b, carry, acc):
                    prev, cur = carry
                    r = pl.multiple_of(b * RB, RB)
                    nxt = pieces(src, z, r + RB)
                    up = pieces(src, zu, r)
                    low = pieces(src, zl, r)
                    o = pieces(o_buf, z, r)
                    ro = pl.multiple_of(r - PAD, RB)
                    for k in range(npc):
                        c = cur[k]
                        west = jnp.where(first_row, pltpu.roll(prev[k], 1, 0), pltpu.roll(c, 1, 0))
                        east = jnp.where(last_row, pltpu.roll(nxt[k], RB - 1, 0), pltpu.roll(c, RB - 1, 0))
                        south = s_buf[pl.ds(r, RB), pl.ds(128 * k, 128)]
                        north = n_buf[pl.ds(r, RB), pl.ds(128 * k, 128)]
                        new = o[k] * (
                            (k0 * c + k_w * west)
                            + (k_e * east + k_s * south)
                            + ((k_n * north + ku * up[k]) + diffusion * low[k])
                        )
                        dst[z, pl.ds(r, RB), pl.ds(128 * k, 128)] = new
                        if acc and k < nacc:
                            sq = new * new
                            if first:
                                out_ref[z, pl.ds(ro, RB), pl.ds(128 * k, 128)] = sq
                            else:
                                out_ref[z, pl.ds(ro, RB), pl.ds(128 * k, 128)] = (
                                    out_ref[z, pl.ds(ro, RB), pl.ds(128 * k, 128)] + sq
                                )
                    return (cur, nxt)

                carry = (pieces(src, z, 0), pieces(src, z, RB))
                if accumulate:
                    carry = lax.fori_loop(b_first, acc_lo, lambda b, c: blk(b, c, False), carry)
                    carry = lax.fori_loop(acc_lo, acc_hi, lambda b, c: blk(b, c, True), carry, unroll=True)
                    carry = lax.fori_loop(acc_hi, b_last + 1, lambda b, c: blk(b, c, False), carry)
                else:
                    carry = lax.fori_loop(b_first, b_last + 1, lambda b, c: blk(b, c, False), carry, unroll=True)

            def lvl_acc(z, c):
                level(z, True)
                return c

            def lvl_plain(z, c):
                level(z, False)
                return c

            lax.fori_loop(0, rz, lvl_acc, 0)
            lax.fori_loop(rz, nz, lvl_plain, 0)

        bufs = (a_buf, b_buf)
        for n in range(STEPS):
            step(bufs[n % 2], bufs[(n + 1) % 2], n == 0)

        def leth(z, c):
            for q in range(nh // 32):
                load = out_ref[z, pl.ds(q * 32, 32), :]
                probit = probit_a + probit_b * jnp.log(load + load_eps)
                lethal = 0.5 * (1.0 + lax.erf((probit - 5.0) / math.sqrt(2.0)))
                out_ref[z, pl.ds(q * 32, 32), :] = weight * lethal
            return c

        lax.fori_loop(0, rz, leth, 0)

    return kernel


def _reduce_sync(weighted):
    count = lax.axis_size("scen")
    parts = weighted.reshape((count, RZ // count) + weighted.shape[1:])
    return lax.all_to_all(parts, "scen", 0, 0, tiled=True).sum(0)


def on_device(source, obstacle, sector, freq_class):
    src = source[0]
    nz, nx, ny = src.shape
    courant_x, courant_y = wind_components(sector[0])
    weight = jnp.exp(-freq_rate * freq_class[0].astype(jnp.float32))
    px = jnp.maximum(courant_x, 0.0)
    mx = jnp.minimum(courant_x, 0.0)
    py = jnp.maximum(courant_y, 0.0)
    my = jnp.minimum(courant_y, 0.0)
    base = 1.0 - px + mx - py + my - 6.0 * diffusion
    coef = jnp.stack(
        [px + diffusion, diffusion - mx, py + diffusion, diffusion - my, base, base - settling,
         weight, jnp.float32(0.0)]
    ).astype(jnp.float32)
    r_lo, r_hi, lanes = ghost_pieces(src, obstacle)
    nh = nx // 2
    rows = nh + 2 * PAD
    width = ny + EXTRA
    any_spec = pl.BlockSpec(memory_space=pl.ANY)
    halves = []
    for half, ghost in ((0, r_lo), (1, r_hi)):
        halves.append(pl.pallas_call(
            make_kernel(nz, nx, ny, RZ, half),
            out_shape=jax.ShapeDtypeStruct((RZ, nh, ny), jnp.float32),
            in_specs=[pl.BlockSpec(memory_space=pltpu.SMEM)] + [any_spec] * 4,
            out_specs=pl.BlockSpec(memory_space=pltpu.VMEM),
            scratch_shapes=[
                pltpu.VMEM((nz, rows, width), jnp.float32),
                pltpu.VMEM((nz, rows, width), jnp.float32),
                pltpu.VMEM((nz, rows, width), jnp.float32),
                pltpu.VMEM((nz, nh + PAD, ny), jnp.int32),
                pltpu.SemaphoreType.DMA((12,)),
                pltpu.VMEM((rows, width), jnp.float32),
                pltpu.VMEM((rows, width), jnp.float32),
            ],
            compiler_params=pltpu.CompilerParams(vmem_limit_bytes=62 * 1024 * 1024),
        )(coef, source, obstacle, ghost, lanes))
        if half == 0:
            first = _reduce_sync(halves[0])
    second = _reduce_sync(halves[1])
    return jnp.concatenate([first, second], axis=1)


def solution(mesh):
    in_specs = (P("scen", None, "gx", "gy"), P(None, "gx", "gy"), P("scen"), P("scen"))
    out_specs = P("scen", "gx", "gy")
    return jax.shard_map(
        on_device, mesh=mesh, in_specs=in_specs, out_specs=out_specs, check_vma=False
    )
```

```python
import math

import jax
import jax.numpy as jnp
from jax import lax
from jax.experimental import pallas as pl
from jax.experimental.pallas import tpu as pltpu
from jax.sharding import PartitionSpec as P

STEPS = 4
RZ = 16


wind_speed = 0.4
diffusion = 0.05
settling = 0.1
probit_a = 3.0
probit_b = 1.0
load_eps = 0.01
freq_rate = 0.7

H = STEPS
PAD = 16
EXTRA = 128
RB = 8


def wind_components(sector_id):
    heading = sector_id.astype(jnp.float32) * (2.0 * math.pi / 16.0)
    return (wind_speed * jnp.cos(heading), wind_speed * jnp.sin(heading))


def _open_and_c(src, obs):
    open_cells = (1 - obs).astype(jnp.float32)
    return jnp.stack([src * open_cells, open_cells])


def _select(count, width, picks):
    cols = jnp.asarray(picks, jnp.int32)[:, None]
    return (lax.broadcasted_iota(jnp.int32, (count, width), 1) == cols).astype(jnp.float32)


def _split3(x):
    def bf(v):
        return lax.reduce_precision(v, exponent_bits=8, mantissa_bits=7)

    top = bf(x)
    rest = x - top
    mid = bf(rest)
    low = rest - mid
    return (top.astype(jnp.bfloat16), mid.astype(jnp.bfloat16), low.astype(jnp.bfloat16))


def ghost_pieces(src, obs):
    nz, nx, ny = src.shape
    gxn = lax.axis_size("gx")
    gyn = lax.axis_size("gy")
    fx = [(i, i + 1) for i in range(gxn - 1)]
    bx = [(i + 1, i) for i in range(gxn - 1)]
    fy = [(i, i + 1) for i in range(gyn - 1)]
    by = [(i + 1, i) for i in range(gyn - 1)]
    hi = lax.Precision.HIGHEST
    last_rows = _open_and_c(src[:, nx - H:, :], obs[:, nx - H:, :])
    first_rows = _open_and_c(src[:, :H, :], obs[:, :H, :])
    xlo = lax.ppermute(last_rows, "gx", fx)
    xhi = lax.ppermute(first_rows, "gx", bx)
    pick = _select(2 * H, ny, list(range(H)) + list(range(ny - H, ny)))
    src_cols = jnp.einsum("zxy,ky->zkx", src, pick, precision=hi)
    open_cols = jnp.einsum(
        "zxy,ky->zkx", (1 - obs).astype(jnp.bfloat16), pick.astype(jnp.bfloat16),
        preferred_element_type=jnp.float32)
    cols = jnp.stack([src_cols * open_cols, open_cols])
    corner_lo = jnp.swapaxes(jnp.concatenate([xlo[..., :H], xlo[..., ny - H:]], -1), -1, -2)
    corner_hi = jnp.swapaxes(jnp.concatenate([xhi[..., :H], xhi[..., ny - H:]], -1), -1, -2)
    ext = jnp.concatenate([corner_lo, cols, corner_hi], axis=-1)
    yw = lax.ppermute(ext[:, :, H:], "gy", fy)
    ye = lax.ppermute(ext[:, :, :H], "gy", by)
    rows = nx + 2 * PAD
    yt = jnp.concatenate([ye, yw], axis=2)
    yt = jnp.pad(yt, ((0, 0), (0, 0), (0, 0), (PAD - H, rows - nx - PAD - H)))
    place = _select(2 * H, EXTRA, list(range(H)) + list(range(EXTRA - H, EXTRA)))
    place = jnp.concatenate([place] * 3, 0).astype(jnp.bfloat16)
    lanes = jnp.einsum(
        "czkr,kj->czrj", jnp.concatenate(_split3(yt), 2), place,
        preferred_element_type=jnp.float32)
    return xlo, xhi, lanes


def make_kernel(nz, nx, ny, rz, half):
    nh = nx // 2
    rows = nh + 2 * PAD
    width = ny + EXTRA
    nblk = rows // RB
    b_first = 1
    b_last = nblk - 2
    acc_lo = PAD // RB
    acc_hi = (PAD + nh) // RB
    nb = nh + PAD
    s0 = 0 if half == 0 else nx - nb
    b0 = PAD if half == 0 else 0
    g0 = PAD - H if half == 0 else nb
    lane0 = 0 if half == 0 else nh

    def kernel(coef, src_hbm, obs_hbm, ghost_hbm, lanes_hbm, out_ref,
               a_buf, b_buf, o_buf, obs_buf, sems, s_buf, n_buf):
        copies = [
            pltpu.make_async_copy(obs_hbm.at[:, pl.ds(s0, nb), :], obs_buf, sems.at[0]),
            pltpu.make_async_copy(ghost_hbm.at[1], o_buf.at[:, pl.ds(g0, H), pl.ds(0, ny)], sems.at[1]),
            pltpu.make_async_copy(lanes_hbm.at[1, :, pl.ds(lane0, rows)], o_buf.at[:, :, pl.ds(ny, EXTRA)], sems.at[3]),
            pltpu.make_async_copy(src_hbm.at[0, :, pl.ds(s0, nb), :], a_buf.at[:, pl.ds(b0, nb), pl.ds(0, ny)], sems.at[4]),
            pltpu.make_async_copy(ghost_hbm.at[0], a_buf.at[:, pl.ds(g0, H), pl.ds(0, ny)], sems.at[5]),
            pltpu.make_async_copy(lanes_hbm.at[0, :, pl.ds(lane0, rows)], a_buf.at[:, :, pl.ds(ny, EXTRA)], sems.at[7]),
        ]
        for cp in copies:
            cp.start()

        zeros = jnp.zeros((RB, width), jnp.float32)

        def clear(z, c):
            b_buf[z, pl.ds(0, RB), :] = zeros
            b_buf[z, pl.ds(rows - RB, RB), :] = zeros
            return c

        lax.fori_loop(0, nz, clear, 0)

        copies[0].wait()

        def to_open(z, c):
            o_buf[z, pl.ds(b0, nb), pl.ds(0, ny)] = (1 - obs_buf[z]).astype(jnp.float32)
            return c

        lax.fori_loop(0, nz, to_open, 0)
        copies[3].wait()

        def to_c0(z, c):
            a_buf[z, pl.ds(b0, nb), pl.ds(0, ny)] = (
                a_buf[z, pl.ds(b0, nb), pl.ds(0, ny)] * o_buf[z, pl.ds(b0, nb), pl.ds(0, ny)]
            )
            return c

        lax.fori_loop(0, nz, to_c0, 0)
        for cp in copies[1:3] + copies[4:]:
            cp.wait()

        k_w = coef[0]
        k_e = coef[1]
        k_s = coef[2]
        k_n = coef[3]
        k0_first = coef[4]
        k0_rest = coef[5]
        weight = coef[6]
        npc = width // 128
        nacc = ny // 128
        row_id = lax.broadcasted_iota(jnp.int32, (RB, 128), 0)
        lane_id = lax.broadcasted_iota(jnp.int32, (RB, 128), 1)
        first_row = row_id == 0
        last_row = row_id == RB - 1
        first_lane = lane_id == 0
        last_lane = lane_id == 127

        def pieces(ref, z, r, count=npc):
            return tuple(ref[z, pl.ds(r, RB), pl.ds(128 * k, 128)] for k in range(count))

        def step(src, dst, first, last):
            nk = nacc if last else npc
            lo_b = acc_lo if last else b_first
            hi_b = acc_hi - 1 if last else b_last
            def level(z, accumulate):
                zu = jnp.minimum(z + 1, nz - 1)
                zl = jnp.maximum(z - 1, 0)
                k0 = jnp.where(z == 0, k0_first, k0_rest)
                ku = jnp.where(z == nz - 1, 0.0, diffusion + settling).astype(jnp.float32)

                def rot(b, c):
                    r = pl.multiple_of(b * RB, RB)
                    cur = pieces(src, z, r)
                    right = tuple(pltpu.roll(v, 1, 1) for v in cur)
                    left = tuple(pltpu.roll(v, 127, 1) for v in cur)
                    for k in range(nk):
                        s_buf[pl.ds(r, RB), pl.ds(128 * k, 128)] = jnp.where(
                            first_lane, right[(k - 1) % npc], right[k])
                        n_buf[pl.ds(r, RB), pl.ds(128 * k, 128)] = jnp.where(
                            last_lane, left[(k + 1) % npc], left[k])
                    return c

                lax.fori_loop(lo_b, hi_b + 1, rot, 0, unroll=True)

                def blk(b, carry, acc):
                    prev, cur = carry
                    r = pl.multiple_of(b * RB, RB)
                    nxt = pieces(src, z, r + RB, nk)
                    up = pieces(src, zu, r, nk)
                    low = pieces(src, zl, r, nk)
                    o = pieces(o_buf, z, r, nk)
                    ro = pl.multiple_of(r - PAD, RB)
                    for k in range(nk):
                        c = cur[k]
                        west = jnp.where(first_row, pltpu.roll(prev[k], 1, 0), pltpu.roll(c, 1, 0))
                        east = jnp.where(last_row, pltpu.roll(nxt[k], RB - 1, 0), pltpu.roll(c, RB - 1, 0))
                        south = s_buf[pl.ds(r, RB), pl.ds(128 * k, 128)]
                        north = n_buf[pl.ds(r, RB), pl.ds(128 * k, 128)]
                        new = o[k] * (
                            (k0 * c + k_w * west)
                            + (k_e * east + k_s * south)
                            + ((k_n * north + ku * up[k]) + diffusion * low[k])
                        )
                        if not last:
                            dst[z, pl.ds(r, RB), pl.ds(128 * k, 128)] = new
                        if acc and k < nacc:
                            sq = new * new
                            if first:
                                out_ref[z, pl.ds(ro, RB), pl.ds(128 * k, 128)] = sq
                            else:
                                out_ref[z, pl.ds(ro, RB), pl.ds(128 * k, 128)] = (
                                    out_ref[z, pl.ds(ro, RB), pl.ds(128 * k, 128)] + sq
                                )
                    return (cur, nxt)

                carry = (pieces(src, z, (lo_b - 1) * RB, nk), pieces(src, z, lo_b * RB, nk))
                if last:
                    lax.fori_loop(acc_lo, acc_hi, lambda b, c: blk(b, c, accumulate), carry, unroll=True)
                elif accumulate:
                    carry = lax.fori_loop(b_first, acc_lo, lambda b, c: blk(b, c, False), carry)
                    carry = lax.fori_loop(acc_lo, acc_hi, lambda b, c: blk(b, c, True), carry, unroll=True)
                    carry = lax.fori_loop(acc_hi, b_last + 1, lambda b, c: blk(b, c, False), carry)
                else:
                    carry = lax.fori_loop(b_first, b_last + 1, lambda b, c: blk(b, c, False), carry, unroll=True)

            def lvl_acc(z, c):
                level(z, True)
                return c

            def lvl_plain(z, c):
                level(z, False)
                return c

            lax.fori_loop(0, rz, lvl_acc, 0)
            lax.fori_loop(rz, nz, lvl_plain, 0)

        bufs = (a_buf, b_buf)
        for n in range(STEPS):
            step(bufs[n % 2], bufs[(n + 1) % 2], n == 0, n == STEPS - 1)

        def leth(z, c):
            for q in range(nh // 32):
                load = out_ref[z, pl.ds(q * 32, 32), :]
                probit = probit_a + probit_b * jnp.log(load + load_eps)
                lethal = 0.5 * (1.0 + lax.erf((probit - 5.0) / math.sqrt(2.0)))
                out_ref[z, pl.ds(q * 32, 32), :] = weight * lethal
            return c

        lax.fori_loop(0, rz, leth, 0)

    return kernel


def _reduce_sync(weighted):
    count = lax.axis_size("scen")
    parts = weighted.reshape((count, RZ // count) + weighted.shape[1:])
    return lax.all_to_all(parts, "scen", 0, 0, tiled=True).sum(0)


def on_device(source, obstacle, sector, freq_class):
    src = source[0]
    nz, nx, ny = src.shape
    courant_x, courant_y = wind_components(sector[0])
    weight = jnp.exp(-freq_rate * freq_class[0].astype(jnp.float32))
    px = jnp.maximum(courant_x, 0.0)
    mx = jnp.minimum(courant_x, 0.0)
    py = jnp.maximum(courant_y, 0.0)
    my = jnp.minimum(courant_y, 0.0)
    base = 1.0 - px + mx - py + my - 6.0 * diffusion
    coef = jnp.stack(
        [px + diffusion, diffusion - mx, py + diffusion, diffusion - my, base, base - settling,
         weight, jnp.float32(0.0)]
    ).astype(jnp.float32)
    r_lo, r_hi, lanes = ghost_pieces(src, obstacle)
    nh = nx // 2
    rows = nh + 2 * PAD
    width = ny + EXTRA
    any_spec = pl.BlockSpec(memory_space=pl.ANY)
    halves = []
    for half, ghost in ((0, r_lo), (1, r_hi)):
        halves.append(pl.pallas_call(
            make_kernel(nz, nx, ny, RZ, half),
            out_shape=jax.ShapeDtypeStruct((RZ, nh, ny), jnp.float32),
            in_specs=[pl.BlockSpec(memory_space=pltpu.SMEM)] + [any_spec] * 4,
            out_specs=pl.BlockSpec(memory_space=pltpu.VMEM),
            scratch_shapes=[
                pltpu.VMEM((nz, rows, width), jnp.float32),
                pltpu.VMEM((nz, rows, width), jnp.float32),
                pltpu.VMEM((nz, rows, width), jnp.float32),
                pltpu.VMEM((nz, nh + PAD, ny), jnp.int32),
                pltpu.SemaphoreType.DMA((8,)),
                pltpu.VMEM((rows, width), jnp.float32),
                pltpu.VMEM((rows, width), jnp.float32),
            ],
            compiler_params=pltpu.CompilerParams(vmem_limit_bytes=62 * 1024 * 1024),
        )(coef, source, obstacle, ghost, lanes))
        if half == 0:
            first = _reduce_sync(halves[0])
    second = _reduce_sync(halves[1])
    return jnp.concatenate([first, second], axis=1)


def solution(mesh):
    in_specs = (P("scen", None, "gx", "gy"), P(None, "gx", "gy"), P("scen"), P("scen"))
    out_specs = P("scen", "gx", "gy")
    return jax.shard_map(
        on_device, mesh=mesh, in_specs=in_specs, out_specs=out_specs, check_vma=False
    )
```

```python
import math

import jax
import jax.numpy as jnp
from jax import lax
from jax.experimental import pallas as pl
from jax.experimental.pallas import tpu as pltpu
from jax.sharding import PartitionSpec as P

STEPS = 4
RZ = 16


wind_speed = 0.4
diffusion = 0.05
settling = 0.1
probit_a = 3.0
probit_b = 1.0
load_eps = 0.01
freq_rate = 0.7

H = STEPS
PAD = 16
EXTRA = 128
RB = 8


def wind_components(sector_id):
    heading = sector_id.astype(jnp.float32) * (2.0 * math.pi / 16.0)
    return (wind_speed * jnp.cos(heading), wind_speed * jnp.sin(heading))


def _open_and_c(src, obs):
    open_cells = (1 - obs).astype(jnp.float32)
    return jnp.stack([src * open_cells, open_cells])


def _select(count, width, picks):
    cols = jnp.asarray(picks, jnp.int32)[:, None]
    return (lax.broadcasted_iota(jnp.int32, (count, width), 1) == cols).astype(jnp.float32)


def _split3(x):
    def bf(v):
        return lax.reduce_precision(v, exponent_bits=8, mantissa_bits=7)

    top = bf(x)
    rest = x - top
    mid = bf(rest)
    low = rest - mid
    return (top.astype(jnp.bfloat16), mid.astype(jnp.bfloat16), low.astype(jnp.bfloat16))


def ghost_pieces(src, obs):
    nz, nx, ny = src.shape
    gxn = lax.axis_size("gx")
    gyn = lax.axis_size("gy")
    fx = [(i, i + 1) for i in range(gxn - 1)]
    bx = [(i + 1, i) for i in range(gxn - 1)]
    fy = [(i, i + 1) for i in range(gyn - 1)]
    by = [(i + 1, i) for i in range(gyn - 1)]
    hi = lax.Precision.HIGHEST
    last_rows = _open_and_c(src[:, nx - H:, :], obs[:, nx - H:, :])
    first_rows = _open_and_c(src[:, :H, :], obs[:, :H, :])
    xlo = lax.ppermute(last_rows, "gx", fx)
    xhi = lax.ppermute(first_rows, "gx", bx)
    pick = _select(2 * H, ny, list(range(H)) + list(range(ny - H, ny)))
    src_cols = jnp.einsum("zxy,ky->zkx", src, pick, precision=hi)
    open_cols = jnp.einsum(
        "zxy,ky->zkx", (1 - obs).astype(jnp.bfloat16), pick.astype(jnp.bfloat16),
        preferred_element_type=jnp.float32)
    cols = jnp.stack([src_cols * open_cols, open_cols])
    corner_lo = jnp.swapaxes(jnp.concatenate([xlo[..., :H], xlo[..., ny - H:]], -1), -1, -2)
    corner_hi = jnp.swapaxes(jnp.concatenate([xhi[..., :H], xhi[..., ny - H:]], -1), -1, -2)
    ext = jnp.concatenate([corner_lo, cols, corner_hi], axis=-1)
    yw = lax.ppermute(ext[:, :, H:], "gy", fy)
    ye = lax.ppermute(ext[:, :, :H], "gy", by)
    rows = nx + 2 * PAD
    yt = jnp.concatenate([ye, yw], axis=2)
    yt = jnp.pad(yt, ((0, 0), (0, 0), (0, 0), (PAD - H, rows - nx - PAD - H)))
    place = _select(2 * H, EXTRA, list(range(H)) + list(range(EXTRA - H, EXTRA)))
    place = jnp.concatenate([place] * 3, 0).astype(jnp.bfloat16)
    lanes = jnp.einsum(
        "czkr,kj->czrj", jnp.concatenate(_split3(yt), 2), place,
        preferred_element_type=jnp.float32)
    return xlo, xhi, lanes


def make_kernel(nz, nx, ny, rz, half):
    nh = nx // 2
    rows = nh + 2 * PAD
    width = ny + EXTRA
    nblk = rows // RB
    b_first = 1
    b_last = nblk - 2
    acc_lo = PAD // RB
    acc_hi = (PAD + nh) // RB
    nb = nh + PAD
    s0 = 0 if half == 0 else nx - nb
    b0 = PAD if half == 0 else 0
    g0 = PAD - H if half == 0 else nb
    lane0 = 0 if half == 0 else nh

    def kernel(coef, src_hbm, obs_hbm, ghost_hbm, lanes_hbm, out_ref,
               a_buf, b_buf, o_buf, obs_buf, sems, s_buf, n_buf):
        copies = [
            pltpu.make_async_copy(obs_hbm.at[:, pl.ds(s0, nb), :], obs_buf, sems.at[0]),
            pltpu.make_async_copy(ghost_hbm.at[1], o_buf.at[:, pl.ds(g0, H), pl.ds(0, ny)], sems.at[1]),
            pltpu.make_async_copy(lanes_hbm.at[1, :, pl.ds(lane0, rows)], o_buf.at[:, :, pl.ds(ny, EXTRA)], sems.at[3]),
            pltpu.make_async_copy(src_hbm.at[0, :, pl.ds(s0, nb), :], a_buf.at[:, pl.ds(b0, nb), pl.ds(0, ny)], sems.at[4]),
            pltpu.make_async_copy(ghost_hbm.at[0], a_buf.at[:, pl.ds(g0, H), pl.ds(0, ny)], sems.at[5]),
            pltpu.make_async_copy(lanes_hbm.at[0, :, pl.ds(lane0, rows)], a_buf.at[:, :, pl.ds(ny, EXTRA)], sems.at[7]),
        ]
        for cp in copies:
            cp.start()

        zeros = jnp.zeros((RB, width), jnp.float32)

        def clear(z, c):
            b_buf[z, pl.ds(0, RB), :] = zeros
            b_buf[z, pl.ds(rows - RB, RB), :] = zeros
            return c

        lax.fori_loop(0, nz, clear, 0)

        copies[0].wait()

        def to_open(z, c):
            o_buf[z, pl.ds(b0, nb), pl.ds(0, ny)] = (1 - obs_buf[z]).astype(jnp.float32)
            return c

        lax.fori_loop(0, nz, to_open, 0)
        copies[3].wait()

        def to_c0(z, c):
            a_buf[z, pl.ds(b0, nb), pl.ds(0, ny)] = (
                a_buf[z, pl.ds(b0, nb), pl.ds(0, ny)] * o_buf[z, pl.ds(b0, nb), pl.ds(0, ny)]
            )
            return c

        lax.fori_loop(0, nz, to_c0, 0)
        for cp in copies[1:3] + copies[4:]:
            cp.wait()

        k_w = coef[0]
        k_e = coef[1]
        k_s = coef[2]
        k_n = coef[3]
        k0_first = coef[4]
        k0_rest = coef[5]
        weight = coef[6]
        npc = width // 128
        nacc = ny // 128
        row_id = lax.broadcasted_iota(jnp.int32, (RB, 128), 0)
        lane_id = lax.broadcasted_iota(jnp.int32, (RB, 128), 1)
        first_row = row_id == 0
        last_row = row_id == RB - 1
        first_lane = lane_id == 0
        last_lane = lane_id == 127

        def pieces(ref, z, r, count=npc):
            return tuple(ref[z, pl.ds(r, RB), pl.ds(128 * k, 128)] for k in range(count))

        def step(src, dst, first, last):
            nk = nacc if last else npc
            lo_b = acc_lo if last else b_first
            hi_b = acc_hi - 1 if last else b_last
            def level(z, accumulate):
                zu = jnp.minimum(z + 1, nz - 1)
                zl = jnp.maximum(z - 1, 0)
                k0 = jnp.where(z == 0, k0_first, k0_rest)
                ku = jnp.where(z == nz - 1, 0.0, diffusion + settling).astype(jnp.float32)

                def rot(b, c):
                    r = pl.multiple_of(b * RB, RB)
                    cur = pieces(src, z, r)
                    right = tuple(pltpu.roll(v, 1, 1) for v in cur)
                    left = tuple(pltpu.roll(v, 127, 1) for v in cur)
                    for k in range(nk):
                        s_buf[pl.ds(r, RB), pl.ds(128 * k, 128)] = jnp.where(
                            first_lane, right[(k - 1) % npc], right[k])
                        n_buf[pl.ds(r, RB), pl.ds(128 * k, 128)] = jnp.where(
                            last_lane, left[(k + 1) % npc], left[k])
                    return c

                lax.fori_loop(lo_b, hi_b + 1, rot, 0, unroll=True)

                def blk(b, carry, acc):
                    prev, cur = carry
                    r = pl.multiple_of(b * RB, RB)
                    nxt = pieces(src, z, r + RB, nk)
                    up = pieces(src, zu, r, nk)
                    low = pieces(src, zl, r, nk)
                    o = pieces(o_buf, z, r, nk)
                    ro = pl.multiple_of(r - PAD, RB)
                    for k in range(nk):
                        c = cur[k]
                        west = jnp.where(first_row, pltpu.roll(prev[k], 1, 0), pltpu.roll(c, 1, 0))
                        east = jnp.where(last_row, pltpu.roll(nxt[k], RB - 1, 0), pltpu.roll(c, RB - 1, 0))
                        south = s_buf[pl.ds(r, RB), pl.ds(128 * k, 128)]
                        north = n_buf[pl.ds(r, RB), pl.ds(128 * k, 128)]
                        new = o[k] * (
                            (k0 * c + k_w * west)
                            + (k_e * east + k_s * south)
                            + ((k_n * north + ku * up[k]) + diffusion * low[k])
                        )
                        if not (last and acc):
                            dst[z, pl.ds(r, RB), pl.ds(128 * k, 128)] = new
                        if acc and k < nacc:
                            sq = new * new
                            if first:
                                out_ref[z, pl.ds(ro, RB), pl.ds(128 * k, 128)] = sq
                            else:
                                out_ref[z, pl.ds(ro, RB), pl.ds(128 * k, 128)] = (
                                    out_ref[z, pl.ds(ro, RB), pl.ds(128 * k, 128)] + sq
                                )
                    return (cur, nxt)

                carry = (pieces(src, z, (lo_b - 1) * RB, nk), pieces(src, z, lo_b * RB, nk))
                if last:
                    lax.fori_loop(acc_lo, acc_hi, lambda b, c: blk(b, c, accumulate), carry, unroll=True)
                elif accumulate:
                    carry = lax.fori_loop(b_first, acc_lo, lambda b, c: blk(b, c, False), carry)
                    carry = lax.fori_loop(acc_lo, acc_hi, lambda b, c: blk(b, c, True), carry, unroll=True)
                    carry = lax.fori_loop(acc_hi, b_last + 1, lambda b, c: blk(b, c, False), carry)
                else:
                    carry = lax.fori_loop(b_first, b_last + 1, lambda b, c: blk(b, c, False), carry, unroll=True)

            def lvl_acc(z, c):
                level(z, True)
                return c

            def lvl_plain(z, c):
                level(z, False)
                return c

            lax.fori_loop(0, rz, lvl_acc, 0)
            lax.fori_loop(rz, nz, lvl_plain, 0)

        bufs = (a_buf, b_buf)
        for n in range(STEPS):
            step(bufs[n % 2], bufs[(n + 1) % 2], n == 0, n == STEPS - 1)

        def leth(z, c):
            for q in range(nh // 32):
                load = out_ref[z, pl.ds(q * 32, 32), :]
                probit = probit_a + probit_b * jnp.log(load + load_eps)
                lethal = 0.5 * (1.0 + lax.erf((probit - 5.0) / math.sqrt(2.0)))
                out_ref[z, pl.ds(q * 32, 32), :] = weight * lethal
            return c

        lax.fori_loop(0, rz, leth, 0)

    return kernel


def _reduce_sync(weighted):
    count = lax.axis_size("scen")
    parts = weighted.reshape((count, RZ // count) + weighted.shape[1:])
    return lax.all_to_all(parts, "scen", 0, 0, tiled=True).sum(0)


def on_device(source, obstacle, sector, freq_class):
    src = source[0]
    nz, nx, ny = src.shape
    courant_x, courant_y = wind_components(sector[0])
    weight = jnp.exp(-freq_rate * freq_class[0].astype(jnp.float32))
    px = jnp.maximum(courant_x, 0.0)
    mx = jnp.minimum(courant_x, 0.0)
    py = jnp.maximum(courant_y, 0.0)
    my = jnp.minimum(courant_y, 0.0)
    base = 1.0 - px + mx - py + my - 6.0 * diffusion
    coef = jnp.stack(
        [px + diffusion, diffusion - mx, py + diffusion, diffusion - my, base, base - settling,
         weight, jnp.float32(0.0)]
    ).astype(jnp.float32)
    r_lo, r_hi, lanes = ghost_pieces(src, obstacle)
    nh = nx // 2
    rows = nh + 2 * PAD
    width = ny + EXTRA
    any_spec = pl.BlockSpec(memory_space=pl.ANY)
    halves = []
    for half, ghost in ((0, r_lo), (1, r_hi)):
        halves.append(pl.pallas_call(
            make_kernel(nz, nx, ny, RZ, half),
            out_shape=jax.ShapeDtypeStruct((RZ, nh, ny), jnp.float32),
            in_specs=[pl.BlockSpec(memory_space=pltpu.SMEM)] + [any_spec] * 4,
            out_specs=pl.BlockSpec(memory_space=pltpu.VMEM),
            scratch_shapes=[
                pltpu.VMEM((nz, rows, width), jnp.float32),
                pltpu.VMEM((nz, rows, width), jnp.float32),
                pltpu.VMEM((nz, rows, width), jnp.float32),
                pltpu.VMEM((nz, nh + PAD, ny), jnp.int32),
                pltpu.SemaphoreType.DMA((8,)),
                pltpu.VMEM((rows, width), jnp.float32),
                pltpu.VMEM((rows, width), jnp.float32),
            ],
            compiler_params=pltpu.CompilerParams(vmem_limit_bytes=62 * 1024 * 1024),
        )(coef, source, obstacle, ghost, lanes))
        if half == 0:
            first = _reduce_sync(halves[0])
    second = _reduce_sync(halves[1])
    return jnp.concatenate([first, second], axis=1)


def solution(mesh):
    in_specs = (P("scen", None, "gx", "gy"), P(None, "gx", "gy"), P("scen"), P("scen"))
    out_specs = P("scen", "gx", "gy")
    return jax.shard_map(
        on_device, mesh=mesh, in_specs=in_specs, out_specs=out_specs, check_vma=False
    )
```
